256 devices in a mesh: req: 64 (over y_lo, z, x), tp: 4 (over y_hi, core).
Axes of the slice: x: 4, y: 4 (y_hi: 2, y_lo: 2; y = y_hi * 2 + y_lo), z: 8, core: 2. Of those that a mesh axis runs over, the one named last changes fastest.
Arguments:
- query_heads: bfloat16 [61440, 4096], P('req', 'tp'), parts along dimension 0, may hold values from -140 to 140
- normed_key_heads: bfloat16 [61440, 512], P('req', 'tp'), parts along dimension 0, may hold values from -7 to 7
- value_rows_per_head: bfloat16 [61440, 512], P('req', 'tp'), parts along dimension 0, may hold values from -6 to 6
- residual_in: bfloat16 [61440, 2048], P(('req', 'tp')), parts along dimension 0, may hold values from -6 to 6
- out_weight: bfloat16 [4096, 2048], P('tp'), may hold values from -0.09375 to 0.09375
- norm_gain: float32 [2048], replicated, may hold values from 0.3 to 3
- gate_up: bfloat16 [2, 2, 2048, 768], P(None, None, None, 'tp'), may hold values from -0.125 to 0.125
- down_weight: bfloat16 [2, 768, 2048], P(None, 'tp'), may hold values from -0.21875 to 0.21875
- segment_ids: int32 [61440], P('req'), parts along dimension 0, may hold values from 0 to 5, never falling along the last dimension, each value on 1 to 480 neighbouring positions
- expert_ids: int32 [61440, 8], P('req'), parts along dimension 0, may hold values from 0 to 127, all different within a row; in each aligned block of 960 rows (0 to 959, 960 to 1919, ...) at most 75 rows name the same one
- gate_weights: float32 [61440, 8], P('req'), parts along dimension 0, may hold values from 0.05 to 0.8
Outputs:
- layer_out: bfloat16 [61440, 2048], P(('req', 'tp')), parts along dimension 0
The draws below stay inside these ranges and needn't reach their ends.
There are 64 independent parts, one for each index of `req`. The reference program is written for one: setup_inputs(seed, part) draws one part's arguments, and reference() takes and returns one part's arrays. A program takes and returns all parts, laid end to end along the dimension named above; an argument that names none is the same for every part. Nothing has to cross between parts.
Inputs may be any that keep to these rules, and one draw needn't show every extreme that they name: `segment_ids`: segment ids never fall along the tokens; each prompt has 1 to 480 tokens and one has exactly 480. `expert_ids`: the 8 experts of a token are distinct; no expert is chosen by more than 75 tokens of a request group, a bound that some block reaches.
All inputs are finite; a program needn't handle non-finite values.
Results may differ from the reference program's by a relative error of at most 0.0053.
Values may be sent and summed in bfloat16 or wider, within the bound.
No kernel may reach another device: no remote copies, remote signals or barrier semaphores. Data moves between devices by JAX's collectives and lax.ppermute only.
A program may use at most 128 MiB of HBM per device.

```python
import math
import jax
import jax.numpy as jnp
import numpy as np
from jax import lax

D = 2048
QUERY_HEADS = 32
KEY_VALUE_HEADS = 4
HEAD_WIDTH = 128
EXPERTS = 128
TOP = 8
FF_E = 768
EXP_WIN = 2
PROMPTS = 6
GROUP_TOKENS = 960
SEG_MOST = 480
CAP = 75


def shared_heads(key):
    rotary_base = jax.random.fold_in(key, 4242)
    sampled_keys = jnp.clip(jax.random.normal(jax.random.fold_in(rotary_base, 1), (GROUP_TOKENS, KEY_VALUE_HEADS * HEAD_WIDTH), jnp.float32), -5.0, 5.0)
    queries_drawn = jnp.clip(jax.random.normal(jax.random.fold_in(rotary_base, 2), (GROUP_TOKENS, QUERY_HEADS * HEAD_WIDTH), jnp.float32), -5.0, 5.0)
    return (sampled_keys, queries_drawn)


def draw_query_heads(key, part):
    return shared_heads(key)[1].astype(jnp.bfloat16)


def draw_normed_key_heads(key, part):
    return shared_heads(key)[0].astype(jnp.bfloat16)


def shard_levels(own_key, dims, pieces, smallest, high):
    factor_of = 1.0
    for position, blocks in pieces:
        heights = jax.random.uniform(jax.random.fold_in(jax.random.fold_in(own_key, 6), position), (blocks,), jnp.float32, smallest / len(pieces), high / len(pieces))
        factor_of = factor_of * jnp.repeat(jnp.exp(heights), dims[position] // blocks).reshape((-1,) + (1,) * (len(dims) - 1 - position))
    return factor_of


def split_up(number_of, total, limit, lean):
    weights = [(1 << 20) // math.isqrt(rank ** lean) + 1 for rank in range(2, number_of + 1)]
    rest, holding = total - limit - (number_of - 1), [1] * (number_of - 1)
    while rest > 0:
        movable = [i for i in range(number_of - 1) if holding[i] < limit]
        mass, budget = sum([weights[i] for i in movable]), rest
        for i in movable:
            more = min(limit - holding[i], max(1, budget * weights[i] // mass), rest)
            holding[i] = holding[i] + more
            rest = rest - more
    return np.array([limit] + holding)


def ragged(own_key, amount, total, limit, lean):
    if amount == 2:
        one = jax.random.randint(own_key, (), max(1, total - limit), min(limit, total - 1) + 1)
        return jnp.stack([one, total - one])
    tallies = jnp.asarray(split_up(amount, total, limit, lean), jnp.int32)
    couples = (amount - 1) // 2
    source_of, sink = tallies[1:1 + 2 * couples:2], tallies[2:2 + 2 * couples:2]
    slack = jnp.minimum(source_of - 1, limit - sink)
    shifted = jax.random.randint(jax.random.fold_in(own_key, 1), (couples,), 0, 1 << 20) % (slack + 1)
    tallies = tallies.at[1:1 + 2 * couples:2].set(source_of - shifted).at[2:2 + 2 * couples:2].set(sink + shifted)
    return tallies[jax.random.permutation(jax.random.fold_in(own_key, 2), amount)]


def shared_out(rng, own, number, rows, amount, top, most, lean):
    ranking = jax.random.permutation(rng, amount)
    packed, usual = shares(amount, rows * top, most, lean, True), shares(amount, rows * top, most, lean, False)
    places = jnp.arange(amount)

    def named(tallies, rotation):
        used = int((tallies > 0).sum())
        fixed = max(1, used // 4)
        shifted = fixed + (places - fixed + rotation * (used - fixed)) % max(1, amount - fixed)
        return jnp.zeros((amount,), jnp.int32).at[ranking[jnp.where(places < fixed, places, shifted)]].set(jnp.asarray(tallies, jnp.int32))

    tallies = jnp.where(number % 4 == 0, named(packed, number // 4), named(usual, number - number // 4 - 1))
    mixed = jax.random.permutation(jax.random.fold_in(own, 3), amount)
    donor, sink = mixed[0:amount // 2 * 2:2], mixed[1:amount // 2 * 2:2]
    slack = jnp.minimum(tallies[donor] - 1, most - tallies[sink]) // 2
    slack = jnp.where((donor == ranking[0]) | (sink == ranking[0]) | (tallies[sink] == 0), 0, jnp.maximum(slack, 0))
    shifted = jax.random.randint(jax.random.fold_in(own, 4), (amount // 2,), 0, 1 << 20) % (slack + 1)
    tallies = tallies.at[donor].add(-shifted).at[sink].add(shifted)
    members = jnp.searchsorted(jnp.cumsum(tallies), jnp.arange(rows * top), side="right").astype(jnp.int32)
    grid = members.reshape(top, rows).T
    grid = grid[jax.random.permutation(jax.random.fold_in(own, 1), rows)]
    rotation = jax.random.randint(jax.random.fold_in(own, 2), (rows, 1), 0, top)
    return jnp.take_along_axis(grid, (jnp.arange(top)[None, :] + rotation) % top, axis=1)


def shares(number_of, total, limit, slope, full):
    portions = [(1 << 20) // math.isqrt(rank ** slope) + 1 for rank in range(1, number_of + 1)]
    largest = limit if full else min(limit, max(-(-total // number_of), total * portions[0] // sum(portions)))
    least = 1 if total - largest >= number_of - 1 else 0
    counts, surplus = [largest] + [least] * (number_of - 1), total - largest - least * (number_of - 1)
    while surplus > 0:
        free = [i for i in range(1, number_of) if counts[i] < largest] or [i for i in range(1, number_of) if counts[i] < limit]
        mass, left = sum([portions[i] for i in free]), surplus
        for i in free:
            extra = min(limit - counts[i], max(1, left * portions[i] // mass), surplus)
            counts[i] = counts[i] + extra
            surplus = surplus - extra
    return np.array(counts)


def centred(rng, shape, width, reach, split=(), held_as=jnp.bfloat16):
    drawn = jax.random.normal(rng, shape, jnp.float32) * width
    if len(split) > 0:
        drawn = shard_levels(rng, shape, split, -0.22, 0.18) * drawn
    return jnp.clip(drawn, min=-reach, max=reach).astype(held_as)


def setup_inputs(seed: int = 0, part: int = 0) -> dict:
    splits = jax.random.split(jax.random.key(seed), 12)
    own_keys = jax.random.split(jax.random.fold_in(splits[11], part), 12)
    query_heads = draw_query_heads(jax.random.fold_in(jax.random.fold_in(splits[11], part), 71), part)
    normed_key_heads = draw_normed_key_heads(jax.random.fold_in(jax.random.fold_in(splits[11], part), 71), part)
    value_rows_per_head = centred(own_keys[2], (GROUP_TOKENS, KEY_VALUE_HEADS * HEAD_WIDTH), 1.0, 6.0, ((1, 4),))
    residual_in = centred(own_keys[3], (GROUP_TOKENS, D), 1.0, 6.0, ((0, 4),))
    out_weight = centred(splits[4], (QUERY_HEADS * HEAD_WIDTH, D), (QUERY_HEADS * HEAD_WIDTH) ** -0.5, 0.09375, ((0, 4),))
    norm_gain = jnp.clip(jnp.exp(jax.random.uniform(splits[5], (D,), jnp.float32, math.log(0.3), math.log(3.0))), 0.3, 3.0)
    gate_up = centred(splits[6], (EXP_WIN, 2, D, FF_E), D ** -0.5, 0.125, ((3, 4),))
    down_weight = centred(splits[7], (EXP_WIN, FF_E, D), FF_E ** -0.5, 0.21875, ((1, 4),))
    segment_ids = jnp.searchsorted(jnp.cumsum(ragged(own_keys[8], PROMPTS, GROUP_TOKENS, SEG_MOST, 2)), jnp.arange(GROUP_TOKENS), side="right").astype(jnp.int32)
    expert_ids_keys = jax.random.split(jax.random.fold_in(own_keys[9], 1), GROUP_TOKENS // GROUP_TOKENS)
    expert_ids_turns = jax.random.permutation(jax.random.fold_in(own_keys[9], 3), GROUP_TOKENS // GROUP_TOKENS)
    expert_ids = jax.vmap(lambda own, number: shared_out(jax.random.fold_in(own_keys[9], 2), own, number, GROUP_TOKENS, EXPERTS, TOP, CAP, 2))(expert_ids_keys, expert_ids_turns).reshape((GROUP_TOKENS, TOP))
    gate_weights = jnp.clip(jnp.exp(jax.random.uniform(own_keys[10], (GROUP_TOKENS, TOP), jnp.float32, math.log(0.05), math.log(0.8))), 0.05, 0.8)
    return dict(query_heads=query_heads, normed_key_heads=normed_key_heads, value_rows_per_head=value_rows_per_head, residual_in=residual_in, out_weight=out_weight, norm_gain=norm_gain, gate_up=gate_up, down_weight=down_weight, segment_ids=segment_ids, expert_ids=expert_ids, gate_weights=gate_weights)


def positions_of(segment_ids):
    earlier = (segment_ids[None, :] < segment_ids[:, None]).astype(jnp.int32)
    return jnp.arange(segment_ids.shape[0], dtype=jnp.int32) - lax.optimization_barrier(jnp.sum(earlier, axis=1)).astype(jnp.int32)

def rotary_tables(vectors, token_positions):
    half_dim = vectors.shape[-1] // 2
    frequency = 1000000.0 ** (-jnp.arange(half_dim, dtype=jnp.float32) / half_dim)
    angles = token_positions.astype(jnp.float32)[:, None] * frequency[None, :]
    cosine = jnp.cos(angles)[:, None, :]
    sine = jnp.sin(angles)[:, None, :]
    first = vectors[..., :half_dim]
    second = vectors[..., half_dim:]
    return jnp.concatenate([first * cosine - second * sine, second * cosine + first * sine], axis=-1)

def rms_norm(hidden, gain):
    widened = hidden.astype(jnp.float32)
    factor = lax.rsqrt(lax.optimization_barrier(jnp.mean(widened * widened, axis=-1, keepdims=True)) + 1e-06)
    return (widened * factor * gain).astype(jnp.bfloat16)

def reference(query_heads, normed_key_heads, value_rows_per_head, residual_in, out_weight, norm_gain, gate_up, down_weight, segment_ids, expert_ids, gate_weights):
    item_count = segment_ids.shape[0]
    token_positions = positions_of(segment_ids)
    query_group_width = QUERY_HEADS // KEY_VALUE_HEADS
    queries = rotary_tables(query_heads.reshape(item_count, QUERY_HEADS, HEAD_WIDTH).astype(jnp.float32), token_positions).astype(jnp.bfloat16)
    keys_after_rotary = rotary_tables(normed_key_heads.reshape(item_count, KEY_VALUE_HEADS, HEAD_WIDTH).astype(jnp.float32), token_positions).astype(jnp.bfloat16)
    head_keys = jnp.repeat(keys_after_rotary, query_group_width, axis=1).transpose(1, 0, 2)
    value_per_head = jnp.repeat(value_rows_per_head.reshape(item_count, KEY_VALUE_HEADS, HEAD_WIDTH), query_group_width, axis=1).transpose(1, 0, 2)
    indices = jnp.arange(item_count)
    allowed = (segment_ids[:, None] == segment_ids[None, :]) & (indices[None, :] <= indices[:, None])
    factor = 1.0 / math.sqrt(HEAD_WIDTH)

    def one_head(operands):
        query_one, key_one, value_one = operands
        scores = jnp.dot(query_one, key_one.T, preferred_element_type=jnp.float32) * factor
        scores = jnp.where(allowed, scores, -1e+30)
        peak = lax.optimization_barrier(jnp.max(scores, axis=1, keepdims=True))
        weights = jnp.exp(scores - peak)
        weights = (weights / lax.optimization_barrier(jnp.sum(weights, axis=1, keepdims=True))).astype(jnp.bfloat16)
        return jnp.dot(weights, value_one, preferred_element_type=jnp.float32).astype(jnp.bfloat16)
    attended = lax.map(one_head, (queries.transpose(1, 0, 2), head_keys, value_per_head))
    attended = attended.transpose(1, 0, 2).reshape(item_count, QUERY_HEADS * HEAD_WIDTH)
    projected = jnp.dot(attended, out_weight, preferred_element_type=jnp.float32)
    mixed = (residual_in.astype(jnp.float32) + projected).astype(jnp.bfloat16)
    normed = rms_norm(mixed, norm_gain)
    slots = jnp.arange(EXP_WIN, dtype=jnp.int32)
    route = lax.optimization_barrier(jnp.sum(jnp.where(expert_ids[:, :, None] == slots[None, None, :], gate_weights[:, :, None], 0.0), axis=1))
    experts = jnp.zeros((item_count, D), jnp.float32)
    for expert in range(EXP_WIN):
        gate = jnp.dot(normed, gate_up[expert, 0], preferred_element_type=jnp.float32)
        upward = jnp.dot(normed, gate_up[expert, 1], preferred_element_type=jnp.float32)
        active = (jax.nn.silu(gate) * upward).astype(jnp.bfloat16)
        experts = experts + route[:, expert:expert + 1] * jnp.dot(active, down_weight[expert], preferred_element_type=jnp.float32)
    return (mixed.astype(jnp.float32) + experts).astype(jnp.bfloat16)
```

```python
import math

import jax
import jax.numpy as jnp
from jax import lax
from jax.sharding import PartitionSpec as P

QUERY_HEADS = 32
KEY_VALUE_HEADS = 4
HEAD_WIDTH = 128
EXPERTS = 128


def positions_of(segment_ids):
    earlier = (segment_ids[None, :] < segment_ids[:, None]).astype(jnp.int32)
    return jnp.arange(segment_ids.shape[0], dtype=jnp.int32) - jnp.sum(earlier, axis=1)


def rotary_tables(vectors, token_positions):
    half_dim = vectors.shape[-1] // 2
    frequency = 1000000.0 ** (-jnp.arange(half_dim, dtype=jnp.float32) / half_dim)
    angles = token_positions.astype(jnp.float32)[:, None] * frequency[None, :]
    cosine = jnp.cos(angles)[:, None, :]
    sine = jnp.sin(angles)[:, None, :]
    first = vectors[..., :half_dim]
    second = vectors[..., half_dim:]
    return jnp.concatenate(
        [first * cosine - second * sine, second * cosine + first * sine], axis=-1
    )


def rms_norm(hidden, gain):
    widened = hidden.astype(jnp.float32)
    factor = lax.rsqrt(jnp.mean(widened * widened, axis=-1, keepdims=True) + 1e-06)
    return (widened * factor * gain).astype(jnp.bfloat16)


def attend(query_heads, normed_key_heads, value_rows_per_head, segment_ids):
    item_count = segment_ids.shape[0]
    token_positions = positions_of(segment_ids)
    kv_local = normed_key_heads.shape[1] // HEAD_WIDTH
    query_group_width = QUERY_HEADS // KEY_VALUE_HEADS
    queries = rotary_tables(
        query_heads.reshape(item_count, kv_local * query_group_width, HEAD_WIDTH).astype(
            jnp.float32
        ),
        token_positions,
    ).astype(jnp.bfloat16)
    keys_after_rotary = rotary_tables(
        normed_key_heads.reshape(item_count, kv_local, HEAD_WIDTH).astype(jnp.float32),
        token_positions,
    ).astype(jnp.bfloat16)
    values = value_rows_per_head.reshape(item_count, kv_local, HEAD_WIDTH)
    indices = jnp.arange(item_count)
    allowed = (segment_ids[:, None] == segment_ids[None, :]) & (
        indices[None, :] <= indices[:, None]
    )
    factor = 1.0 / math.sqrt(HEAD_WIDTH)
    key_one = keys_after_rotary[:, 0]
    value_one = values[:, 0]

    def one_head(query_one, key_one=key_one, value_one=value_one):
        scores = jnp.dot(query_one, key_one.T, preferred_element_type=jnp.float32) * factor
        scores = jnp.where(allowed, scores, -1e30)
        peak = jnp.max(scores, axis=1, keepdims=True)
        weights = jnp.exp(scores - peak)
        weights = (weights / jnp.sum(weights, axis=1, keepdims=True)).astype(jnp.bfloat16)
        return jnp.dot(weights, value_one, preferred_element_type=jnp.float32).astype(jnp.bfloat16)

    group_queries = queries.transpose(1, 0, 2)
    blocks = lax.map(one_head, group_queries)
    attended = blocks.transpose(1, 0, 2)
    return attended.reshape(item_count, kv_local * query_group_width * HEAD_WIDTH)


def local(
    query_heads,
    normed_key_heads,
    value_rows_per_head,
    residual_in,
    out_weight,
    norm_gain,
    gate_up,
    down_weight,
    segment_ids,
    expert_ids,
    gate_weights,
):
    attended = attend(query_heads, normed_key_heads, value_rows_per_head, segment_ids)
    tok_rows = residual_in.shape[0]
    group_tokens = expert_ids.shape[0]
    capacity = min(group_tokens * expert_ids.shape[1] * 5 // (EXPERTS * 4), group_tokens)
    window = gate_up.shape[0]
    slots = jnp.arange(window, dtype=jnp.int32)
    hits = expert_ids[:, :, None] == slots[None, None, :]
    route_all = jnp.sum(jnp.where(hits, gate_weights[:, :, None], 0.0), axis=1)
    chosen = jnp.any(hits, axis=1)
    rank = jnp.cumsum(chosen.astype(jnp.int32), axis=0) - 1
    kk = jnp.arange(capacity, dtype=jnp.int32)
    select_all = (rank.T[:, None, :] == kk[None, :, None]) & chosen.T[:, None, :]
    route_sel = jnp.sum(jnp.where(select_all, route_all.T[:, None, :], 0.0), axis=-1)
    first = lax.axis_index("tp") * tok_rows
    select_loc = lax.dynamic_slice_in_dim(select_all, first, tok_rows, axis=2)

    partial = jnp.dot(attended, out_weight, preferred_element_type=jnp.float32)
    projected = lax.psum_scatter(
        partial.astype(jnp.bfloat16), "tp", scatter_dimension=0, tiled=True
    )
    mixed = (residual_in.astype(jnp.float32) + projected.astype(jnp.float32)).astype(jnp.bfloat16)
    normed = rms_norm(mixed, norm_gain)

    picked_own = jnp.einsum(
        "ekt,td->ekd", select_loc.astype(jnp.bfloat16), normed,
        preferred_element_type=jnp.float32,
    ).astype(jnp.bfloat16)
    picked = lax.psum(picked_own, "tp")
    gate = jnp.einsum("ekd,edf->ekf", picked, gate_up[:, 0], preferred_element_type=jnp.float32)
    upward = jnp.einsum("ekd,edf->ekf", picked, gate_up[:, 1], preferred_element_type=jnp.float32)
    active = (jax.nn.silu(gate) * upward).astype(jnp.bfloat16)
    outputs = jnp.einsum("ekf,efd->ekd", active, down_weight, preferred_element_type=jnp.float32)
    scaled = lax.psum(route_sel[:, :, None] * outputs, "tp")
    experts = jnp.einsum(
        "ekt,ekd->td", select_loc.astype(jnp.float32), scaled,
        precision=lax.Precision.HIGHEST, preferred_element_type=jnp.float32,
    )
    return (mixed.astype(jnp.float32) + experts).astype(jnp.bfloat16)


def solution(mesh):
    placed = (
        P("req", "tp"),
        P("req", "tp"),
        P("req", "tp"),
        P(("req", "tp"), None),
        P("tp", None),
        P(),
        P(None, None, None, "tp"),
        P(None, "tp", None),
        P("req"),
        P("req", None),
        P("req", None),
    )
    return jax.shard_map(
        local, mesh=mesh, in_specs=placed, out_specs=P(("req", "tp"), None), check_vma=False
    )
```

```python
import math

import jax
import jax.numpy as jnp
from jax import lax
from jax.sharding import PartitionSpec as P

QUERY_HEADS = 32
KEY_VALUE_HEADS = 4
HEAD_WIDTH = 128
EXPERTS = 128


def positions_of(segment_ids):
    earlier = (segment_ids[None, :] < segment_ids[:, None]).astype(jnp.int32)
    return jnp.arange(segment_ids.shape[0], dtype=jnp.int32) - jnp.sum(earlier, axis=1)


def rotary_tables(vectors, token_positions):
    half_dim = vectors.shape[-1] // 2
    frequency = 1000000.0 ** (-jnp.arange(half_dim, dtype=jnp.float32) / half_dim)
    angles = token_positions.astype(jnp.float32)[:, None] * frequency[None, :]
    cosine = jnp.cos(angles)[:, None, :]
    sine = jnp.sin(angles)[:, None, :]
    first = vectors[..., :half_dim]
    second = vectors[..., half_dim:]
    return jnp.concatenate(
        [first * cosine - second * sine, second * cosine + first * sine], axis=-1
    )


def rms_norm(hidden, gain):
    widened = hidden.astype(jnp.float32)
    factor = lax.rsqrt(jnp.mean(widened * widened, axis=-1, keepdims=True) + 1e-06)
    return (widened * factor * gain).astype(jnp.bfloat16)


SEG_MOST = 480


def xor_pairs(size, mask):
    return [(index, index ^ mask) for index in range(size)]


def attend_block(query_rows, first, keys_after_rotary, values, segment_ids, token_positions):
    rows = query_rows.shape[0]
    item_count = segment_ids.shape[0]
    span = min(item_count, rows + SEG_MOST)
    head_count = query_rows.shape[1] // HEAD_WIDTH
    start = jnp.clip(first + rows - span, 0, item_count - span)
    row_index = first + jnp.arange(rows, dtype=jnp.int32)
    key_index = start + jnp.arange(span, dtype=jnp.int32)
    row_segment = lax.dynamic_slice_in_dim(segment_ids, first, rows)
    key_segment = lax.dynamic_slice_in_dim(segment_ids, start, span)
    allowed = (row_segment[:, None] == key_segment[None, :]) & (
        key_index[None, :] <= row_index[:, None]
    )
    key_one = lax.dynamic_slice_in_dim(keys_after_rotary, start, span)
    value_one = lax.dynamic_slice_in_dim(values, start, span)
    queries = rotary_tables(
        query_rows.reshape(rows, head_count, HEAD_WIDTH).astype(jnp.float32),
        lax.dynamic_slice_in_dim(token_positions, first, rows),
    ).astype(jnp.bfloat16)
    factor = 1.0 / math.sqrt(HEAD_WIDTH)

    def one_head(query_one):
        scores = jnp.dot(query_one, key_one.T, preferred_element_type=jnp.float32) * factor
        scores = jnp.where(allowed, scores, -1e30)
        peak = jnp.max(scores, axis=1, keepdims=True)
        weights = jnp.exp(scores - peak)
        weights = (weights / jnp.sum(weights, axis=1, keepdims=True)).astype(jnp.bfloat16)
        return jnp.dot(weights, value_one, preferred_element_type=jnp.float32).astype(jnp.bfloat16)

    blocks = lax.map(one_head, queries.transpose(1, 0, 2))
    return blocks.transpose(1, 0, 2).reshape(rows, head_count * HEAD_WIDTH)


def local(
    query_heads,
    normed_key_heads,
    value_rows_per_head,
    residual_in,
    out_weight,
    norm_gain,
    gate_up,
    down_weight,
    segment_ids,
    expert_ids,
    gate_weights,
):
    tok_rows = residual_in.shape[0]
    group_tokens = expert_ids.shape[0]
    size = lax.axis_size("tp")
    me = lax.axis_index("tp")
    token_positions = positions_of(segment_ids)
    keys_after_rotary = rotary_tables(
        normed_key_heads.reshape(group_tokens, 1, HEAD_WIDTH).astype(jnp.float32), token_positions
    ).astype(jnp.bfloat16)[:, 0]
    values = value_rows_per_head

    def projected_block(block):
        first = block * tok_rows
        query_rows = lax.dynamic_slice_in_dim(query_heads, first, tok_rows)
        attended = attend_block(
            query_rows, first, keys_after_rotary, values, segment_ids, token_positions
        )
        return jnp.dot(attended, out_weight, preferred_element_type=jnp.float32)

    to_partner = jnp.stack([projected_block(me ^ 1), projected_block(me ^ 3)]).astype(jnp.bfloat16)
    from_partner = lax.ppermute(to_partner, "tp", xor_pairs(size, 1))
    across = projected_block(me ^ 2) + from_partner[1].astype(jnp.float32)
    from_across = lax.ppermute(across.astype(jnp.bfloat16), "tp", xor_pairs(size, 2))
    projected = (
        projected_block(me)
        + from_partner[0].astype(jnp.float32)
        + from_across.astype(jnp.float32)
    )
    mixed = (residual_in.astype(jnp.float32) + projected).astype(jnp.bfloat16)
    normed = rms_norm(mixed, norm_gain)

    capacity = min(group_tokens * expert_ids.shape[1] * 5 // (EXPERTS * 4), group_tokens)
    window = gate_up.shape[0]
    slots = jnp.arange(window, dtype=jnp.int32)
    hits = expert_ids[:, :, None] == slots[None, None, :]
    route_all = jnp.sum(jnp.where(hits, gate_weights[:, :, None], 0.0), axis=1)
    chosen = jnp.any(hits, axis=1)
    rank = jnp.cumsum(chosen.astype(jnp.int32), axis=0) - 1
    kk = jnp.arange(capacity, dtype=jnp.int32)
    select_all = (rank.T[:, None, :] == kk[None, :, None]) & chosen.T[:, None, :]
    route_sel = jnp.sum(jnp.where(select_all, route_all.T[:, None, :], 0.0), axis=-1)
    select_loc = lax.dynamic_slice_in_dim(select_all, me * tok_rows, tok_rows, axis=2)

    picked = jnp.einsum(
        "ekt,td->ekd", select_loc.astype(jnp.bfloat16), normed,
        preferred_element_type=jnp.float32,
    ).astype(jnp.bfloat16)
    picked = picked + lax.ppermute(picked, "tp", xor_pairs(size, 1))
    picked = picked + lax.ppermute(picked, "tp", xor_pairs(size, 2))
    gate = jnp.einsum("ekd,edf->ekf", picked, gate_up[:, 0], preferred_element_type=jnp.float32)
    upward = jnp.einsum("ekd,edf->ekf", picked, gate_up[:, 1], preferred_element_type=jnp.float32)
    active = (jax.nn.silu(gate) * upward).astype(jnp.bfloat16)
    outputs = jnp.einsum("ekf,efd->ekd", active, down_weight, preferred_element_type=jnp.float32)
    scaled = route_sel[:, :, None] * outputs
    scaled = scaled + lax.ppermute(scaled, "tp", xor_pairs(size, 1))
    scaled = scaled + lax.ppermute(
        scaled.astype(jnp.bfloat16), "tp", xor_pairs(size, 2)
    ).astype(jnp.float32)
    experts = jnp.einsum(
        "ekt,ekd->td", select_loc.astype(jnp.float32), scaled,
        precision=lax.Precision.HIGHEST, preferred_element_type=jnp.float32,
    )
    return (mixed.astype(jnp.float32) + experts).astype(jnp.bfloat16)


def solution(mesh):
    placed = (
        P("req", "tp"),
        P("req", "tp"),
        P("req", "tp"),
        P(("req", "tp"), None),
        P("tp", None),
        P(),
        P(None, None, None, "tp"),
        P(None, "tp", None),
        P("req"),
        P("req", None),
        P("req", None),
    )
    return jax.shard_map(
        local, mesh=mesh, in_specs=placed, out_specs=P(("req", "tp"), None), check_vma=False
    )
```

```python
import math

import jax
import jax.numpy as jnp
from jax import lax
from jax.sharding import PartitionSpec as P

QUERY_HEADS = 32
KEY_VALUE_HEADS = 4
HEAD_WIDTH = 128
EXPERTS = 128


def positions_of(segment_ids):
    earlier = (segment_ids[None, :] < segment_ids[:, None]).astype(jnp.int32)
    return jnp.arange(segment_ids.shape[0], dtype=jnp.int32) - jnp.sum(earlier, axis=1)


def rotary_tables(vectors, token_positions):
    half_dim = vectors.shape[-1] // 2
    frequency = 1000000.0 ** (-jnp.arange(half_dim, dtype=jnp.float32) / half_dim)
    angles = token_positions.astype(jnp.float32)[:, None] * frequency[None, :]
    cosine = jnp.cos(angles)[:, None, :]
    sine = jnp.sin(angles)[:, None, :]
    first = vectors[..., :half_dim]
    second = vectors[..., half_dim:]
    return jnp.concatenate(
        [first * cosine - second * sine, second * cosine + first * sine], axis=-1
    )


def rms_norm(hidden, gain):
    widened = hidden.astype(jnp.float32)
    factor = lax.rsqrt(jnp.mean(widened * widened, axis=-1, keepdims=True) + 1e-06)
    return (widened * factor * gain).astype(jnp.bfloat16)


SEG_MOST = 480


def xor_pairs(size, mask):
    return [(index, index ^ mask) for index in range(size)]


def attend_blocks(query_heads, firsts, rows, keys_after_rotary, values, segment_ids, token_positions):
    item_count = segment_ids.shape[0]
    span = min(item_count, rows + SEG_MOST)
    head_count = query_heads.shape[1] // HEAD_WIDTH
    starts = [jnp.clip(first + rows - span, 0, item_count - span) for first in firsts]
    row_index = jnp.stack([first + jnp.arange(rows, dtype=jnp.int32) for first in firsts])
    key_index = jnp.stack([start + jnp.arange(span, dtype=jnp.int32) for start in starts])
    row_segment = jnp.stack([lax.dynamic_slice_in_dim(segment_ids, f, rows) for f in firsts])
    key_segment = jnp.stack([lax.dynamic_slice_in_dim(segment_ids, s, span) for s in starts])
    allowed = (row_segment[:, :, None] == key_segment[:, None, :]) & (
        key_index[:, None, :] <= row_index[:, :, None]
    )
    key_one = jnp.stack([lax.dynamic_slice_in_dim(keys_after_rotary, s, span) for s in starts])
    value_one = jnp.stack([lax.dynamic_slice_in_dim(values, s, span) for s in starts])
    query_rows = jnp.concatenate([lax.dynamic_slice_in_dim(query_heads, f, rows) for f in firsts])
    row_positions = jnp.concatenate(
        [lax.dynamic_slice_in_dim(token_positions, f, rows) for f in firsts]
    )
    queries = rotary_tables(
        query_rows.reshape(len(firsts) * rows, head_count, HEAD_WIDTH).astype(jnp.float32),
        row_positions,
    ).astype(jnp.bfloat16)
    factor = 1.0 / math.sqrt(HEAD_WIDTH)
    stacked = queries.reshape(len(firsts), rows * head_count, HEAD_WIDTH)
    scores = jnp.einsum(
        "nqd,nkd->nqk", stacked, key_one, preferred_element_type=jnp.float32
    ) * factor
    scores = scores.reshape(len(firsts), rows, head_count, span)
    scores = jnp.where(allowed[:, :, None, :], scores, -1e30)
    peak = jnp.max(scores, axis=3, keepdims=True)
    weights = jnp.exp(scores - peak)
    weights = (weights / jnp.sum(weights, axis=3, keepdims=True)).astype(jnp.bfloat16)
    attended = jnp.einsum(
        "nqk,nkd->nqd",
        weights.reshape(len(firsts), rows * head_count, span),
        value_one,
        preferred_element_type=jnp.float32,
    ).astype(jnp.bfloat16)
    return attended.reshape(len(firsts), rows, head_count * HEAD_WIDTH)


def local(
    query_heads,
    normed_key_heads,
    value_rows_per_head,
    residual_in,
    out_weight,
    norm_gain,
    gate_up,
    down_weight,
    segment_ids,
    expert_ids,
    gate_weights,
):
    tok_rows = residual_in.shape[0]
    group_tokens = expert_ids.shape[0]
    size = lax.axis_size("tp")
    me = lax.axis_index("tp")
    token_positions = positions_of(segment_ids)
    keys_after_rotary = rotary_tables(
        normed_key_heads.reshape(group_tokens, 1, HEAD_WIDTH).astype(jnp.float32), token_positions
    ).astype(jnp.bfloat16)[:, 0]
    values = value_rows_per_head

    def projected_blocks(blocks, queries):
        attended = attend_blocks(
            queries, [block * tok_rows for block in blocks], tok_rows,
            keys_after_rotary, values, segment_ids, token_positions,
        )
        return jnp.einsum(
            "nrc,cd->nrd", attended, out_weight, preferred_element_type=jnp.float32
        )

    first_pair = projected_blocks([me ^ 3, me ^ 2], query_heads)
    partner_cross = lax.ppermute(first_pair[0].astype(jnp.bfloat16), "tp", xor_pairs(size, 1))
    across = (first_pair[1] + partner_cross.astype(jnp.float32)).astype(jnp.bfloat16)
    across, later_queries = lax.optimization_barrier((across, query_heads))
    from_across = lax.ppermute(across, "tp", xor_pairs(size, 2))
    second_pair = projected_blocks([me ^ 1, me], later_queries)
    partner_own = lax.ppermute(second_pair[0].astype(jnp.bfloat16), "tp", xor_pairs(size, 1))
    projected = (
        second_pair[1]
        + partner_own.astype(jnp.float32)
        + from_across.astype(jnp.float32)
    )
    mixed = (residual_in.astype(jnp.float32) + projected).astype(jnp.bfloat16)
    normed = rms_norm(mixed, norm_gain)

    capacity = min(group_tokens * expert_ids.shape[1] * 5 // (EXPERTS * 4), group_tokens)
    window = gate_up.shape[0]
    slots = jnp.arange(window, dtype=jnp.int32)
    hits = expert_ids[:, :, None] == slots[None, None, :]
    route_all = jnp.sum(jnp.where(hits, gate_weights[:, :, None], 0.0), axis=1)
    chosen = jnp.any(hits, axis=1)
    rank = jnp.cumsum(chosen.astype(jnp.int32), axis=0) - 1
    kk = jnp.arange(capacity, dtype=jnp.int32)
    select_all = (rank.T[:, None, :] == kk[None, :, None]) & chosen.T[:, None, :]
    route_sel = jnp.sum(jnp.where(select_all, route_all.T[:, None, :], 0.0), axis=-1)
    select_loc = lax.dynamic_slice_in_dim(select_all, me * tok_rows, tok_rows, axis=2)

    picked = jnp.einsum(
        "ekt,td->ekd", select_loc.astype(jnp.bfloat16), normed,
        preferred_element_type=jnp.float32,
    ).astype(jnp.bfloat16)
    picked = picked + lax.ppermute(picked, "tp", xor_pairs(size, 1))
    picked = picked + lax.ppermute(picked, "tp", xor_pairs(size, 2))
    gate = jnp.einsum("ekd,edf->ekf", picked, gate_up[:, 0], preferred_element_type=jnp.float32)
    upward = jnp.einsum("ekd,edf->ekf", picked, gate_up[:, 1], preferred_element_type=jnp.float32)
    active = (jax.nn.silu(gate) * upward).astype(jnp.bfloat16)
    outputs = jnp.einsum("ekf,efd->ekd", active, down_weight, preferred_element_type=jnp.float32)
    scaled = route_sel[:, :, None] * outputs
    scaled = scaled + lax.ppermute(scaled, "tp", xor_pairs(size, 1))
    scaled = scaled + lax.ppermute(
        scaled.astype(jnp.bfloat16), "tp", xor_pairs(size, 2)
    ).astype(jnp.float32)
    experts = jnp.einsum(
        "ekt,ekd->td", select_loc.astype(jnp.float32), scaled,
        precision=lax.Precision.HIGHEST, preferred_element_type=jnp.float32,
    )
    return (mixed.astype(jnp.float32) + experts).astype(jnp.bfloat16)


def solution(mesh):
    placed = (
        P("req", "tp"),
        P("req", "tp"),
        P("req", "tp"),
        P(("req", "tp"), None),
        P("tp", None),
        P(),
        P(None, None, None, "tp"),
        P(None, "tp", None),
        P("req"),
        P("req", None),
        P("req", None),
    )
    return jax.shard_map(
        local, mesh=mesh, in_specs=placed, out_specs=P(("req", "tp"), None), check_vma=False
    )
```

```python
import math

import jax
import jax.numpy as jnp
from jax import lax
from jax.sharding import PartitionSpec as P

QUERY_HEADS = 32
KEY_VALUE_HEADS = 4
HEAD_WIDTH = 128
EXPERTS = 128


def positions_of(segment_ids):
    earlier = (segment_ids[None, :] < segment_ids[:, None]).astype(jnp.int32)
    return jnp.arange(segment_ids.shape[0], dtype=jnp.int32) - jnp.sum(earlier, axis=1)


def rotary_tables(vectors, token_positions):
    half_dim = vectors.shape[-1] // 2
    frequency = 1000000.0 ** (-jnp.arange(half_dim, dtype=jnp.float32) / half_dim)
    angles = token_positions.astype(jnp.float32)[:, None] * frequency[None, :]
    cosine = jnp.cos(angles)[:, None, :]
    sine = jnp.sin(angles)[:, None, :]
    first = vectors[..., :half_dim]
    second = vectors[..., half_dim:]
    return jnp.concatenate(
        [first * cosine - second * sine, second * cosine + first * sine], axis=-1
    )


def rms_norm(hidden, gain):
    widened = hidden.astype(jnp.float32)
    factor = lax.rsqrt(jnp.mean(widened * widened, axis=-1, keepdims=True) + 1e-06)
    return (widened * factor * gain).astype(jnp.bfloat16)


SEG_MOST = 480


def xor_pairs(size, mask):
    return [(index, index ^ mask) for index in range(size)]


def attend_blocks(query_heads, firsts, rows, keys_after_rotary, values, segment_ids, token_positions):
    item_count = segment_ids.shape[0]
    span = min(item_count, rows + SEG_MOST)
    head_count = query_heads.shape[1] // HEAD_WIDTH
    starts = [jnp.clip(first + rows - span, 0, item_count - span) for first in firsts]
    row_index = jnp.stack([first + jnp.arange(rows, dtype=jnp.int32) for first in firsts])
    key_index = jnp.stack([start + jnp.arange(span, dtype=jnp.int32) for start in starts])
    row_segment = jnp.stack([lax.dynamic_slice_in_dim(segment_ids, f, rows) for f in firsts])
    key_segment = jnp.stack([lax.dynamic_slice_in_dim(segment_ids, s, span) for s in starts])
    allowed = (row_segment[:, :, None] == key_segment[:, None, :]) & (
        key_index[:, None, :] <= row_index[:, :, None]
    )
    key_one = jnp.stack([lax.dynamic_slice_in_dim(keys_after_rotary, s, span) for s in starts])
    value_one = jnp.stack([lax.dynamic_slice_in_dim(values, s, span) for s in starts])
    query_rows = jnp.concatenate([lax.dynamic_slice_in_dim(query_heads, f, rows) for f in firsts])
    row_positions = jnp.concatenate(
        [lax.dynamic_slice_in_dim(token_positions, f, rows) for f in firsts]
    )
    queries = rotary_tables(
        query_rows.reshape(len(firsts) * rows, head_count, HEAD_WIDTH).astype(jnp.float32),
        row_positions,
    ).astype(jnp.bfloat16)
    factor = 1.0 / math.sqrt(HEAD_WIDTH)
    queries = queries.reshape(len(firsts), rows, head_count, HEAD_WIDTH)
    scores = jnp.einsum(
        "nqhd,nkd->nhqk", queries, key_one, preferred_element_type=jnp.float32
    ) * factor
    scores = jnp.where(allowed[:, None, :, :], scores, -1e30)
    peak = jnp.max(scores, axis=3, keepdims=True)
    weights = jnp.exp(scores - peak)
    weights = (weights / jnp.sum(weights, axis=3, keepdims=True)).astype(jnp.bfloat16)
    return jnp.einsum(
        "nhqk,nkd->nhqd", weights, value_one, preferred_element_type=jnp.float32
    ).astype(jnp.bfloat16)


def local(
    query_heads,
    normed_key_heads,
    value_rows_per_head,
    residual_in,
    out_weight,
    norm_gain,
    gate_up,
    down_weight,
    segment_ids,
    expert_ids,
    gate_weights,
):
    tok_rows = residual_in.shape[0]
    group_tokens = expert_ids.shape[0]
    size = lax.axis_size("tp")
    me = lax.axis_index("tp")
    token_positions = positions_of(segment_ids)
    keys_after_rotary = rotary_tables(
        normed_key_heads.reshape(group_tokens, 1, HEAD_WIDTH).astype(jnp.float32), token_positions
    ).astype(jnp.bfloat16)[:, 0]
    values = value_rows_per_head

    def projected_blocks(blocks, queries):
        attended = attend_blocks(
            queries, [block * tok_rows for block in blocks], tok_rows,
            keys_after_rotary, values, segment_ids, token_positions,
        )
        head_count = attended.shape[1]
        return jnp.einsum(
            "nhrc,hcd->nrd", attended, out_weight.reshape(head_count, HEAD_WIDTH, -1),
            preferred_element_type=jnp.float32,
        )

    first_pair = projected_blocks([me ^ 3, me ^ 2], query_heads)
    partner_cross = lax.ppermute(first_pair[0].astype(jnp.bfloat16), "tp", xor_pairs(size, 1))
    across = (first_pair[1] + partner_cross.astype(jnp.float32)).astype(jnp.bfloat16)
    across, later_queries = lax.optimization_barrier((across, query_heads))
    from_across = lax.ppermute(across, "tp", xor_pairs(size, 2))
    second_pair = projected_blocks([me ^ 1, me], later_queries)
    partner_own = lax.ppermute(second_pair[0].astype(jnp.bfloat16), "tp", xor_pairs(size, 1))
    projected = (
        second_pair[1]
        + partner_own.astype(jnp.float32)
        + from_across.astype(jnp.float32)
    )
    mixed = (residual_in.astype(jnp.float32) + projected).astype(jnp.bfloat16)
    normed = rms_norm(mixed, norm_gain)

    capacity = min(group_tokens * expert_ids.shape[1] * 5 // (EXPERTS * 4), group_tokens)
    window = gate_up.shape[0]
    slots = jnp.arange(window, dtype=jnp.int32)
    hits = expert_ids[:, :, None] == slots[None, None, :]
    route_all = jnp.sum(jnp.where(hits, gate_weights[:, :, None], 0.0), axis=1)
    chosen = jnp.any(hits, axis=1)
    rank = jnp.cumsum(chosen.astype(jnp.int32), axis=0) - 1
    kk = jnp.arange(capacity, dtype=jnp.int32)
    select_all = (rank.T[:, None, :] == kk[None, :, None]) & chosen.T[:, None, :]
    route_sel = jnp.sum(jnp.where(select_all, route_all.T[:, None, :], 0.0), axis=-1)
    select_loc = lax.dynamic_slice_in_dim(select_all, me * tok_rows, tok_rows, axis=2)

    picked = jnp.einsum(
        "ekt,td->ekd", select_loc.astype(jnp.bfloat16), normed,
        preferred_element_type=jnp.float32,
    ).astype(jnp.bfloat16)
    picked = picked + lax.ppermute(picked, "tp", xor_pairs(size, 1))
    picked = picked + lax.ppermute(picked, "tp", xor_pairs(size, 2))
    gate = jnp.einsum("ekd,edf->ekf", picked, gate_up[:, 0], preferred_element_type=jnp.float32)
    upward = jnp.einsum("ekd,edf->ekf", picked, gate_up[:, 1], preferred_element_type=jnp.float32)
    active = (jax.nn.silu(gate) * upward).astype(jnp.bfloat16)
    outputs = jnp.einsum("ekf,efd->ekd", active, down_weight, preferred_element_type=jnp.float32)
    scaled = route_sel[:, :, None] * outputs
    scaled = scaled + lax.ppermute(scaled, "tp", xor_pairs(size, 1))
    scaled = scaled + lax.ppermute(
        scaled.astype(jnp.bfloat16), "tp", xor_pairs(size, 2)
    ).astype(jnp.float32)
    experts = jnp.einsum(
        "ekt,ekd->td", select_loc.astype(jnp.float32), scaled,
        precision=lax.Precision.HIGHEST, preferred_element_type=jnp.float32,
    )
    return (mixed.astype(jnp.float32) + experts).astype(jnp.bfloat16)


def solution(mesh):
    placed = (
        P("req", "tp"),
        P("req", "tp"),
        P("req", "tp"),
        P(("req", "tp"), None),
        P("tp", None),
        P(),
        P(None, None, None, "tp"),
        P(None, "tp", None),
        P("req"),
        P("req", None),
        P("req", None),
    )
    return jax.shard_map(
        local, mesh=mesh, in_specs=placed, out_specs=P(("req", "tp"), None), check_vma=False
    )
```

```python
import math

import jax
import jax.numpy as jnp
from jax import lax
from jax.sharding import PartitionSpec as P

QUERY_HEADS = 32
KEY_VALUE_HEADS = 4
HEAD_WIDTH = 128
EXPERTS = 128


def positions_of(segment_ids):
    earlier = (segment_ids[None, :] < segment_ids[:, None]).astype(jnp.int32)
    return jnp.arange(segment_ids.shape[0], dtype=jnp.int32) - jnp.sum(earlier, axis=1)


def rotary_tables(vectors, token_positions):
    half_dim = vectors.shape[-1] // 2
    frequency = 1000000.0 ** (-jnp.arange(half_dim, dtype=jnp.float32) / half_dim)
    angles = token_positions.astype(jnp.float32)[:, None] * frequency[None, :]
    cosine = jnp.cos(angles)[:, None, :]
    sine = jnp.sin(angles)[:, None, :]
    first = vectors[..., :half_dim]
    second = vectors[..., half_dim:]
    return jnp.concatenate(
        [first * cosine - second * sine, second * cosine + first * sine], axis=-1
    )


def rms_norm(hidden, gain):
    widened = hidden.astype(jnp.float32)
    factor = lax.rsqrt(jnp.mean(widened * widened, axis=-1, keepdims=True) + 1e-06)
    return (widened * factor * gain).astype(jnp.bfloat16)


SEG_MOST = 480


def xor_pairs(size, mask):
    return [(index, index ^ mask) for index in range(size)]


def attend_blocks(query_heads, firsts, rows, keys_after_rotary, values, segment_ids, token_positions):
    item_count = segment_ids.shape[0]
    span = min(item_count, rows + SEG_MOST)
    head_count = query_heads.shape[1] // HEAD_WIDTH
    starts = [jnp.clip(first + rows - span, 0, item_count - span) for first in firsts]
    row_index = jnp.stack([first + jnp.arange(rows, dtype=jnp.int32) for first in firsts])
    key_index = jnp.stack([start + jnp.arange(span, dtype=jnp.int32) for start in starts])
    row_segment = jnp.stack([lax.dynamic_slice_in_dim(segment_ids, f, rows) for f in firsts])
    key_segment = jnp.stack([lax.dynamic_slice_in_dim(segment_ids, s, span) for s in starts])
    key_one = jnp.stack([lax.dynamic_slice_in_dim(keys_after_rotary, s, span) for s in starts])
    value_one = jnp.stack([lax.dynamic_slice_in_dim(values, s, span) for s in starts])
    query_rows = jnp.concatenate([lax.dynamic_slice_in_dim(query_heads, f, rows) for f in firsts])
    row_positions = jnp.concatenate(
        [lax.dynamic_slice_in_dim(token_positions, f, rows) for f in firsts]
    )
    queries = rotary_tables(
        query_rows.reshape(len(firsts) * rows, head_count, HEAD_WIDTH).astype(jnp.float32),
        row_positions,
    ).astype(jnp.bfloat16)
    factor = 1.0 / math.sqrt(HEAD_WIDTH)
    stacked = queries.reshape(len(firsts), rows * head_count, HEAD_WIDTH)
    scores = jnp.einsum(
        "nqd,nkd->nqk", stacked, key_one, preferred_element_type=jnp.float32
    ) * factor
    stacked_segment = jnp.repeat(row_segment, head_count, axis=1)
    stacked_index = jnp.repeat(row_index, head_count, axis=1)
    allowed = (stacked_segment[:, :, None] == key_segment[:, None, :]) & (
        key_index[:, None, :] <= stacked_index[:, :, None]
    )
    scores = jnp.where(allowed, scores, -1e30)
    peak = jnp.max(scores, axis=2, keepdims=True)
    weights = jnp.exp(scores - peak)
    weights = (weights / jnp.sum(weights, axis=2, keepdims=True)).astype(jnp.bfloat16)
    attended = jnp.einsum(
        "nqk,nkd->nqd",
        weights,
        value_one,
        preferred_element_type=jnp.float32,
    ).astype(jnp.bfloat16)
    return attended.reshape(len(firsts), rows, head_count * HEAD_WIDTH)


def local(
    query_heads,
    normed_key_heads,
    value_rows_per_head,
    residual_in,
    out_weight,
    norm_gain,
    gate_up,
    down_weight,
    segment_ids,
    expert_ids,
    gate_weights,
):
    tok_rows = residual_in.shape[0]
    group_tokens = expert_ids.shape[0]
    size = lax.axis_size("tp")
    me = lax.axis_index("tp")
    token_positions = positions_of(segment_ids)
    keys_after_rotary = rotary_tables(
        normed_key_heads.reshape(group_tokens, 1, HEAD_WIDTH).astype(jnp.float32), token_positions
    ).astype(jnp.bfloat16)[:, 0]
    values = value_rows_per_head

    def projected_blocks(blocks, queries):
        attended = attend_blocks(
            queries, [block * tok_rows for block in blocks], tok_rows,
            keys_after_rotary, values, segment_ids, token_positions,
        )
        return jnp.einsum(
            "nrc,cd->nrd", attended, out_weight, preferred_element_type=jnp.float32
        )

    first_pair = projected_blocks([me ^ 3, me ^ 2], query_heads)
    partner_cross = lax.ppermute(first_pair[0].astype(jnp.bfloat16), "tp", xor_pairs(size, 1))
    across = first_pair[1] + partner_cross.astype(jnp.float32)
    across, later_queries = lax.optimization_barrier((across, query_heads))
    from_across = lax.ppermute(across, "tp", xor_pairs(size, 2))
    second_pair = projected_blocks([me ^ 1, me], later_queries)
    partner_own = lax.ppermute(second_pair[0].astype(jnp.bfloat16), "tp", xor_pairs(size, 1))
    projected = (
        second_pair[1]
        + partner_own.astype(jnp.float32)
        + from_across.astype(jnp.float32)
    )
    mixed = (residual_in.astype(jnp.float32) + projected).astype(jnp.bfloat16)
    normed = rms_norm(mixed, norm_gain)

    capacity = min(group_tokens * expert_ids.shape[1] * 5 // (EXPERTS * 4), group_tokens)
    window = gate_up.shape[0]
    slots = jnp.arange(window, dtype=jnp.int32)
    hits = expert_ids[:, :, None] == slots[None, None, :]
    route_all = jnp.sum(jnp.where(hits, gate_weights[:, :, None], 0.0), axis=1)
    chosen = jnp.any(hits, axis=1)
    rank = jnp.cumsum(chosen.astype(jnp.int32), axis=0) - 1
    kk = jnp.arange(capacity, dtype=jnp.int32)
    select_all = (rank.T[:, None, :] == kk[None, :, None]) & chosen.T[:, None, :]
    route_sel = jnp.sum(jnp.where(select_all, route_all.T[:, None, :], 0.0), axis=-1)
    select_loc = lax.dynamic_slice_in_dim(select_all, me * tok_rows, tok_rows, axis=2)

    picked = jnp.einsum(
        "ekt,td->ekd", select_loc.astype(jnp.bfloat16), normed,
        preferred_element_type=jnp.float32,
    ).astype(jnp.bfloat16)
    picked = picked + lax.ppermute(picked, "tp", xor_pairs(size, 1))
    picked = picked + lax.ppermute(picked, "tp", xor_pairs(size, 2))
    gate = jnp.einsum("ekd,edf->ekf", picked, gate_up[:, 0], preferred_element_type=jnp.float32)
    upward = jnp.einsum("ekd,edf->ekf", picked, gate_up[:, 1], preferred_element_type=jnp.float32)
    active = (jax.nn.silu(gate) * upward).astype(jnp.bfloat16)
    outputs = jnp.einsum("ekf,efd->ekd", active, down_weight, preferred_element_type=jnp.float32)
    scaled = route_sel[:, :, None] * outputs
    scaled = scaled + lax.ppermute(scaled, "tp", xor_pairs(size, 1))
    scaled = scaled + lax.ppermute(
        scaled.astype(jnp.bfloat16), "tp", xor_pairs(size, 2)
    ).astype(jnp.float32)
    experts = jnp.einsum(
        "ekt,ekd->td", select_loc.astype(jnp.float32), scaled,
        precision=lax.Precision.HIGHEST, preferred_element_type=jnp.float32,
    )
    return (mixed.astype(jnp.float32) + experts).astype(jnp.bfloat16)


def solution(mesh):
    placed = (
        P("req", "tp"),
        P("req", "tp"),
        P("req", "tp"),
        P(("req", "tp"), None),
        P("tp", None),
        P(),
        P(None, None, None, "tp"),
        P(None, "tp", None),
        P("req"),
        P("req", None),
        P("req", None),
    )
    return jax.shard_map(
        local, mesh=mesh, in_specs=placed, out_specs=P(("req", "tp"), None), check_vma=False
    )
```

```python
import math

import jax
import jax.numpy as jnp
from jax import lax
from jax.sharding import PartitionSpec as P

QUERY_HEADS = 32
KEY_VALUE_HEADS = 4
HEAD_WIDTH = 128
EXPERTS = 128


def positions_of(segment_ids):
    earlier = (segment_ids[None, :] < segment_ids[:, None]).astype(jnp.int32)
    return jnp.arange(segment_ids.shape[0], dtype=jnp.int32) - jnp.sum(earlier, axis=1)


def rotary_tables(vectors, token_positions):
    half_dim = vectors.shape[-1] // 2
    frequency = 1000000.0 ** (-jnp.arange(half_dim, dtype=jnp.float32) / half_dim)
    angles = token_positions.astype(jnp.float32)[:, None] * frequency[None, :]
    cosine = jnp.cos(angles)[:, None, :]
    sine = jnp.sin(angles)[:, None, :]
    first = vectors[..., :half_dim]
    second = vectors[..., half_dim:]
    return jnp.concatenate(
        [first * cosine - second * sine, second * cosine + first * sine], axis=-1
    )


def rms_norm(hidden, gain):
    widened = hidden.astype(jnp.float32)
    factor = lax.rsqrt(jnp.mean(widened * widened, axis=-1, keepdims=True) + 1e-06)
    return (widened * factor * gain).astype(jnp.bfloat16)


SEG_MOST = 480


def xor_pairs(size, mask):
    return [(index, index ^ mask) for index in range(size)]


def attend_blocks(query_heads, firsts, rows, keys_after_rotary, values, segment_ids, token_positions):
    item_count = segment_ids.shape[0]
    span = min(item_count, rows + SEG_MOST)
    head_count = query_heads.shape[1] // HEAD_WIDTH
    starts = [jnp.clip(first + rows - span, 0, item_count - span) for first in firsts]
    row_index = jnp.stack([first + jnp.arange(rows, dtype=jnp.int32) for first in firsts])
    key_index = jnp.stack([start + jnp.arange(span, dtype=jnp.int32) for start in starts])
    row_segment = jnp.stack([lax.dynamic_slice_in_dim(segment_ids, f, rows) for f in firsts])
    key_segment = jnp.stack([lax.dynamic_slice_in_dim(segment_ids, s, span) for s in starts])
    allowed = (row_segment[:, :, None] == key_segment[:, None, :]) & (
        key_index[:, None, :] <= row_index[:, :, None]
    )
    key_one = jnp.stack([lax.dynamic_slice_in_dim(keys_after_rotary, s, span) for s in starts])
    value_one = jnp.stack([lax.dynamic_slice_in_dim(values, s, span) for s in starts])
    query_rows = jnp.concatenate([lax.dynamic_slice_in_dim(query_heads, f, rows) for f in firsts])
    row_positions = jnp.concatenate(
        [lax.dynamic_slice_in_dim(token_positions, f, rows) for f in firsts]
    )
    queries = rotary_tables(
        query_rows.reshape(len(firsts) * rows, head_count, HEAD_WIDTH).astype(jnp.float32),
        row_positions,
    ).astype(jnp.bfloat16)
    factor = 1.0 / math.sqrt(HEAD_WIDTH)
    stacked = queries.reshape(len(firsts), rows * head_count, HEAD_WIDTH)
    scores = jnp.einsum(
        "nqd,nkd->nqk", stacked, key_one, preferred_element_type=jnp.float32
    ) * factor
    scores = scores.reshape(len(firsts), rows, head_count, span)
    scores = jnp.where(allowed[:, :, None, :], scores, -1e30)
    peak = jnp.max(scores, axis=3, keepdims=True)
    weights = jnp.exp(scores - peak)
    weights = (weights / jnp.sum(weights, axis=3, keepdims=True)).astype(jnp.bfloat16)
    attended = jnp.einsum(
        "nqk,nkd->nqd",
        weights.reshape(len(firsts), rows * head_count, span),
        value_one,
        preferred_element_type=jnp.float32,
    ).astype(jnp.bfloat16)
    return attended.reshape(len(firsts), rows, head_count * HEAD_WIDTH)


def attend_selected(queries_raw, rows_index, rows_segment, rows_position, keys_after_rotary,
                    values, segment_ids):
    rows = queries_raw.shape[0]
    item_count = segment_ids.shape[0]
    head_count = queries_raw.shape[1] // HEAD_WIDTH
    queries = rotary_tables(
        queries_raw.reshape(rows, head_count, HEAD_WIDTH).astype(jnp.float32), rows_position
    ).astype(jnp.bfloat16)
    factor = 1.0 / math.sqrt(HEAD_WIDTH)
    stacked = queries.reshape(rows * head_count, HEAD_WIDTH)
    scores = jnp.dot(stacked, keys_after_rotary.T, preferred_element_type=jnp.float32) * factor
    stacked_segment = jnp.repeat(rows_segment, head_count)
    stacked_index = jnp.repeat(rows_index, head_count)
    key_index = jnp.arange(item_count, dtype=jnp.int32)
    allowed = (stacked_segment[:, None] == segment_ids[None, :]) & (
        key_index[None, :] <= stacked_index[:, None]
    )
    scores = jnp.where(allowed, scores, -1e30)
    peak = jnp.max(scores, axis=1, keepdims=True)
    weights = jnp.exp(scores - peak)
    weights = (weights / jnp.sum(weights, axis=1, keepdims=True)).astype(jnp.bfloat16)
    attended = jnp.dot(weights, values, preferred_element_type=jnp.float32).astype(jnp.bfloat16)
    return attended.reshape(rows, head_count * HEAD_WIDTH)


def local(
    query_heads,
    normed_key_heads,
    value_rows_per_head,
    residual_in,
    out_weight,
    norm_gain,
    gate_up,
    down_weight,
    segment_ids,
    expert_ids,
    gate_weights,
):
    tok_rows = residual_in.shape[0]
    group_tokens = expert_ids.shape[0]
    size = lax.axis_size("tp")
    me = lax.axis_index("tp")
    token_positions = positions_of(segment_ids)
    keys_after_rotary = rotary_tables(
        normed_key_heads.reshape(group_tokens, 1, HEAD_WIDTH).astype(jnp.float32), token_positions
    ).astype(jnp.bfloat16)[:, 0]
    values = value_rows_per_head

    capacity = min(group_tokens * expert_ids.shape[1] * 5 // (EXPERTS * 4), group_tokens)
    window = gate_up.shape[0]
    slots = jnp.arange(window, dtype=jnp.int32)
    hits = expert_ids[:, :, None] == slots[None, None, :]
    route_all = jnp.sum(jnp.where(hits, gate_weights[:, :, None], 0.0), axis=1)
    chosen = jnp.any(hits, axis=1)
    rank = jnp.cumsum(chosen.astype(jnp.int32), axis=0) - 1
    kk = jnp.arange(capacity, dtype=jnp.int32)
    select_all = (rank.T[:, None, :] == kk[None, :, None]) & chosen.T[:, None, :]
    route_sel = jnp.sum(jnp.where(select_all, route_all.T[:, None, :], 0.0), axis=-1)
    select_loc = lax.dynamic_slice_in_dim(select_all, me * tok_rows, tok_rows, axis=2)

    picked_count = window * capacity
    select_flat = select_all.reshape(picked_count, group_tokens)
    valid = jnp.any(select_flat, axis=1)
    token_index = jnp.arange(group_tokens, dtype=jnp.int32)
    rows_index = jnp.sum(jnp.where(select_flat, token_index[None, :], 0), axis=1)
    rows_segment = jnp.where(
        valid, jnp.sum(jnp.where(select_flat, segment_ids[None, :], 0), axis=1), -1
    )
    rows_position = jnp.sum(jnp.where(select_flat, token_positions[None, :], 0), axis=1)
    queries_sel = jnp.dot(
        select_flat.astype(jnp.bfloat16), query_heads, preferred_element_type=jnp.float32
    ).astype(jnp.bfloat16)
    attended_sel = attend_selected(
        queries_sel, rows_index, rows_segment, rows_position, keys_after_rotary, values,
        segment_ids,
    )
    residual_sel = jnp.dot(
        select_loc.reshape(picked_count, tok_rows).astype(jnp.bfloat16), residual_in,
        preferred_element_type=jnp.float32,
    )
    summed_sel = residual_sel + jnp.dot(
        attended_sel, out_weight, preferred_element_type=jnp.float32
    )
    summed_sel = summed_sel + lax.ppermute(summed_sel, "tp", xor_pairs(size, 1))
    summed_sel = summed_sel + lax.ppermute(
        summed_sel.astype(jnp.bfloat16), "tp", xor_pairs(size, 2)
    ).astype(jnp.float32)
    picked = rms_norm(summed_sel.astype(jnp.bfloat16), norm_gain)
    picked = picked.reshape(window, capacity, -1)
    gate = jnp.einsum("ekd,edf->ekf", picked, gate_up[:, 0], preferred_element_type=jnp.float32)
    upward = jnp.einsum("ekd,edf->ekf", picked, gate_up[:, 1], preferred_element_type=jnp.float32)
    active = (jax.nn.silu(gate) * upward).astype(jnp.bfloat16)
    outputs = jnp.einsum("ekf,efd->ekd", active, down_weight, preferred_element_type=jnp.float32)
    scaled = route_sel[:, :, None] * outputs
    scaled = scaled + lax.ppermute(scaled, "tp", xor_pairs(size, 1))
    scaled = scaled + lax.ppermute(
        scaled.astype(jnp.bfloat16), "tp", xor_pairs(size, 2)
    ).astype(jnp.float32)
    experts = jnp.einsum(
        "ekt,ekd->td", select_loc.astype(jnp.float32), scaled,
        precision=lax.Precision.HIGHEST, preferred_element_type=jnp.float32,
    )

    def projected_blocks(blocks, queries):
        attended = attend_blocks(
            queries, [block * tok_rows for block in blocks], tok_rows,
            keys_after_rotary, values, segment_ids, token_positions,
        )
        return jnp.einsum(
            "nrc,cd->nrd", attended, out_weight, preferred_element_type=jnp.float32
        )

    first_pair = projected_blocks([me ^ 3, me ^ 2], query_heads)
    partner_cross = lax.ppermute(first_pair[0].astype(jnp.bfloat16), "tp", xor_pairs(size, 1))
    across = (first_pair[1] + partner_cross.astype(jnp.float32)).astype(jnp.bfloat16)
    across, later_queries = lax.optimization_barrier((across, query_heads))
    from_across = lax.ppermute(across, "tp", xor_pairs(size, 2))
    second_pair = projected_blocks([me ^ 1, me], later_queries)
    partner_own = lax.ppermute(second_pair[0].astype(jnp.bfloat16), "tp", xor_pairs(size, 1))
    projected = (
        second_pair[1]
        + partner_own.astype(jnp.float32)
        + from_across.astype(jnp.float32)
    )
    mixed = (residual_in.astype(jnp.float32) + projected).astype(jnp.bfloat16)
    return (mixed.astype(jnp.float32) + experts).astype(jnp.bfloat16)


def solution(mesh):
    placed = (
        P("req", "tp"),
        P("req", "tp"),
        P("req", "tp"),
        P(("req", "tp"), None),
        P("tp", None),
        P(),
        P(None, None, None, "tp"),
        P(None, "tp", None),
        P("req"),
        P("req", None),
        P("req", None),
    )
    return jax.shard_map(
        local, mesh=mesh, in_specs=placed, out_specs=P(("req", "tp"), None), check_vma=False
    )
```

```python
import math

import jax
import jax.numpy as jnp
from jax import lax
from jax.sharding import PartitionSpec as P

QUERY_HEADS = 32
KEY_VALUE_HEADS = 4
HEAD_WIDTH = 128
EXPERTS = 128


def positions_of(segment_ids):
    earlier = (segment_ids[None, :] < segment_ids[:, None]).astype(jnp.int32)
    return jnp.arange(segment_ids.shape[0], dtype=jnp.int32) - jnp.sum(earlier, axis=1)


def rotary_tables(vectors, token_positions):
    half_dim = vectors.shape[-1] // 2
    frequency = 1000000.0 ** (-jnp.arange(half_dim, dtype=jnp.float32) / half_dim)
    angles = token_positions.astype(jnp.float32)[:, None] * frequency[None, :]
    cosine = jnp.cos(angles)[:, None, :]
    sine = jnp.sin(angles)[:, None, :]
    first = vectors[..., :half_dim]
    second = vectors[..., half_dim:]
    return jnp.concatenate(
        [first * cosine - second * sine, second * cosine + first * sine], axis=-1
    )


def rms_norm(hidden, gain):
    widened = hidden.astype(jnp.float32)
    factor = lax.rsqrt(jnp.mean(widened * widened, axis=-1, keepdims=True) + 1e-06)
    return (widened * factor * gain).astype(jnp.bfloat16)


SEG_MOST = 480


def xor_pairs(size, mask):
    return [(index, index ^ mask) for index in range(size)]


def attend_blocks(
    query_heads, firsts, rows, keys_after_rotary, values, segment_ids, token_positions, per_row
):
    item_count = segment_ids.shape[0]
    span = min(item_count, rows + SEG_MOST)
    head_count = query_heads.shape[1] // HEAD_WIDTH
    starts = [jnp.clip(first + rows - span, 0, item_count - span) for first in firsts]
    row_index = jnp.stack([first + jnp.arange(rows, dtype=jnp.int32) for first in firsts])
    key_index = jnp.stack([start + jnp.arange(span, dtype=jnp.int32) for start in starts])
    row_segment = jnp.stack([lax.dynamic_slice_in_dim(segment_ids, f, rows) for f in firsts])
    key_segment = jnp.stack([lax.dynamic_slice_in_dim(segment_ids, s, span) for s in starts])
    allowed = (row_segment[:, :, None] == key_segment[:, None, :]) & (
        key_index[:, None, :] <= row_index[:, :, None]
    )
    key_one = jnp.stack([lax.dynamic_slice_in_dim(keys_after_rotary, s, span) for s in starts])
    value_one = jnp.stack([lax.dynamic_slice_in_dim(values, s, span) for s in starts])
    query_rows = jnp.concatenate([lax.dynamic_slice_in_dim(query_heads, f, rows) for f in firsts])
    row_positions = jnp.concatenate(
        [lax.dynamic_slice_in_dim(token_positions, f, rows) for f in firsts]
    )
    queries = rotary_tables(
        query_rows.reshape(len(firsts) * rows, head_count, HEAD_WIDTH).astype(jnp.float32),
        row_positions,
    ).astype(jnp.bfloat16)
    factor = 1.0 / math.sqrt(HEAD_WIDTH)
    stacked = queries.reshape(len(firsts), rows * head_count, HEAD_WIDTH)
    scores = jnp.einsum(
        "nqd,nkd->nqk", stacked, key_one, preferred_element_type=jnp.float32
    ) * factor
    if per_row:
        stacked_segment = jnp.repeat(row_segment, head_count, axis=1)
        stacked_index = jnp.repeat(row_index, head_count, axis=1)
        stacked_allowed = (stacked_segment[:, :, None] == key_segment[:, None, :]) & (
            key_index[:, None, :] <= stacked_index[:, :, None]
        )
        scores = jnp.where(stacked_allowed, scores, -1e30)
        peak = jnp.max(scores, axis=2, keepdims=True)
        weights = jnp.exp(scores - peak)
        weights = (weights / jnp.sum(weights, axis=2, keepdims=True)).astype(jnp.bfloat16)
    else:
        scores = scores.reshape(len(firsts), rows, head_count, span)
        scores = jnp.where(allowed[:, :, None, :], scores, -1e30)
        peak = jnp.max(scores, axis=3, keepdims=True)
        weights = jnp.exp(scores - peak)
        weights = (weights / jnp.sum(weights, axis=3, keepdims=True)).astype(jnp.bfloat16)
    attended = jnp.einsum(
        "nqk,nkd->nqd",
        weights.reshape(len(firsts), rows * head_count, span),
        value_one,
        preferred_element_type=jnp.float32,
    ).astype(jnp.bfloat16)
    return attended.reshape(len(firsts), rows, head_count * HEAD_WIDTH)


def local(
    query_heads,
    normed_key_heads,
    value_rows_per_head,
    residual_in,
    out_weight,
    norm_gain,
    gate_up,
    down_weight,
    segment_ids,
    expert_ids,
    gate_weights,
):
    tok_rows = residual_in.shape[0]
    group_tokens = expert_ids.shape[0]
    size = lax.axis_size("tp")
    me = lax.axis_index("tp")
    token_positions = positions_of(segment_ids)
    keys_after_rotary = rotary_tables(
        normed_key_heads.reshape(group_tokens, 1, HEAD_WIDTH).astype(jnp.float32), token_positions
    ).astype(jnp.bfloat16)[:, 0]
    values = value_rows_per_head

    def projected_blocks(blocks, queries, per_row):
        attended = attend_blocks(
            queries, [block * tok_rows for block in blocks], tok_rows,
            keys_after_rotary, values, segment_ids, token_positions, per_row,
        )
        return jnp.einsum(
            "nrc,cd->nrd", attended, out_weight, preferred_element_type=jnp.float32
        )

    first_pair = projected_blocks([me ^ 3, me ^ 2], query_heads, True)
    partner_cross = lax.ppermute(first_pair[0].astype(jnp.bfloat16), "tp", xor_pairs(size, 1))
    across = (first_pair[1] + partner_cross.astype(jnp.float32)).astype(jnp.bfloat16)
    across, later_queries = lax.optimization_barrier((across, query_heads))
    from_across = lax.ppermute(across, "tp", xor_pairs(size, 2))
    second_pair = projected_blocks([me ^ 1, me], later_queries, False)
    partner_own = lax.ppermute(second_pair[0].astype(jnp.bfloat16), "tp", xor_pairs(size, 1))
    projected = (
        second_pair[1]
        + partner_own.astype(jnp.float32)
        + from_across.astype(jnp.float32)
    )
    mixed = (residual_in.astype(jnp.float32) + projected).astype(jnp.bfloat16)
    normed = rms_norm(mixed, norm_gain)

    capacity = min(group_tokens * expert_ids.shape[1] * 5 // (EXPERTS * 4), group_tokens)
    window = gate_up.shape[0]
    slots = jnp.arange(window, dtype=jnp.int32)
    hits = expert_ids[:, :, None] == slots[None, None, :]
    route_all = jnp.sum(jnp.where(hits, gate_weights[:, :, None], 0.0), axis=1)
    chosen = jnp.any(hits, axis=1)
    rank = jnp.cumsum(chosen.astype(jnp.int32), axis=0) - 1
    kk = jnp.arange(capacity, dtype=jnp.int32)
    select_all = (rank.T[:, None, :] == kk[None, :, None]) & chosen.T[:, None, :]
    route_sel = jnp.sum(jnp.where(select_all, route_all.T[:, None, :], 0.0), axis=-1)
    select_loc = lax.dynamic_slice_in_dim(select_all, me * tok_rows, tok_rows, axis=2)

    picked = jnp.einsum(
        "ekt,td->ekd", select_loc.astype(jnp.bfloat16), normed,
        preferred_element_type=jnp.float32,
    ).astype(jnp.bfloat16)
    picked = picked + lax.ppermute(picked, "tp", xor_pairs(size, 1))
    picked = picked + lax.ppermute(picked, "tp", xor_pairs(size, 2))
    gate = jnp.einsum("ekd,edf->ekf", picked, gate_up[:, 0], preferred_element_type=jnp.float32)
    upward = jnp.einsum("ekd,edf->ekf", picked, gate_up[:, 1], preferred_element_type=jnp.float32)
    active = (jax.nn.silu(gate) * upward).astype(jnp.bfloat16)
    outputs = jnp.einsum("ekf,efd->ekd", active, down_weight, preferred_element_type=jnp.float32)
    scaled = route_sel[:, :, None] * outputs
    scaled = scaled + lax.ppermute(scaled, "tp", xor_pairs(size, 1))
    scaled = scaled + lax.ppermute(
        scaled.astype(jnp.bfloat16), "tp", xor_pairs(size, 2)
    ).astype(jnp.float32)
    experts = jnp.einsum(
        "ekt,ekd->td", select_loc.astype(jnp.float32), scaled,
        precision=lax.Precision.HIGHEST, preferred_element_type=jnp.float32,
    )
    return (mixed.astype(jnp.float32) + experts).astype(jnp.bfloat16)


def solution(mesh):
    placed = (
        P("req", "tp"),
        P("req", "tp"),
        P("req", "tp"),
        P(("req", "tp"), None),
        P("tp", None),
        P(),
        P(None, None, None, "tp"),
        P(None, "tp", None),
        P("req"),
        P("req", None),
        P("req", None),
    )
    return jax.shard_map(
        local, mesh=mesh, in_specs=placed, out_specs=P(("req", "tp"), None), check_vma=False
    )
```

```python
import math

import jax
import jax.numpy as jnp
from jax import lax
from jax.sharding import PartitionSpec as P

QUERY_HEADS = 32
KEY_VALUE_HEADS = 4
HEAD_WIDTH = 128
EXPERTS = 128


def positions_of(segment_ids):
    earlier = (segment_ids[None, :] < segment_ids[:, None]).astype(jnp.int32)
    return jnp.arange(segment_ids.shape[0], dtype=jnp.int32) - jnp.sum(earlier, axis=1)


def rotary_tables(vectors, token_positions):
    half_dim = vectors.shape[-1] // 2
    frequency = 1000000.0 ** (-jnp.arange(half_dim, dtype=jnp.float32) / half_dim)
    angles = token_positions.astype(jnp.float32)[:, None] * frequency[None, :]
    cosine = jnp.cos(angles)[:, None, :]
    sine = jnp.sin(angles)[:, None, :]
    first = vectors[..., :half_dim]
    second = vectors[..., half_dim:]
    return jnp.concatenate(
        [first * cosine - second * sine, second * cosine + first * sine], axis=-1
    )


def rms_norm(hidden, gain):
    widened = hidden.astype(jnp.float32)
    factor = lax.rsqrt(jnp.mean(widened * widened, axis=-1, keepdims=True) + 1e-06)
    return (widened * factor * gain).astype(jnp.bfloat16)


SEG_MOST = 480


def xor_pairs(size, mask):
    return [(index, index ^ mask) for index in range(size)]


def attend_blocks(
    query_heads, firsts, rows, keys_after_rotary, values, segment_ids, token_positions, per_row
):
    item_count = segment_ids.shape[0]
    span = min(item_count, rows + SEG_MOST)
    head_count = query_heads.shape[1] // HEAD_WIDTH
    starts = [jnp.clip(first + rows - span, 0, item_count - span) for first in firsts]
    row_index = jnp.stack([first + jnp.arange(rows, dtype=jnp.int32) for first in firsts])
    key_index = jnp.stack([start + jnp.arange(span, dtype=jnp.int32) for start in starts])
    row_segment = jnp.stack([lax.dynamic_slice_in_dim(segment_ids, f, rows) for f in firsts])
    key_segment = jnp.stack([lax.dynamic_slice_in_dim(segment_ids, s, span) for s in starts])
    allowed = (row_segment[:, :, None] == key_segment[:, None, :]) & (
        key_index[:, None, :] <= row_index[:, :, None]
    )
    key_one = jnp.stack([lax.dynamic_slice_in_dim(keys_after_rotary, s, span) for s in starts])
    value_one = jnp.stack([lax.dynamic_slice_in_dim(values, s, span) for s in starts])
    query_rows = jnp.concatenate([lax.dynamic_slice_in_dim(query_heads, f, rows) for f in firsts])
    row_positions = jnp.concatenate(
        [lax.dynamic_slice_in_dim(token_positions, f, rows) for f in firsts]
    )
    queries = rotary_tables(
        query_rows.reshape(len(firsts) * rows, head_count, HEAD_WIDTH).astype(jnp.float32),
        row_positions,
    ).astype(jnp.bfloat16)
    factor = 1.0 / math.sqrt(HEAD_WIDTH)
    stacked = queries.reshape(len(firsts), rows * head_count, HEAD_WIDTH)
    scores = jnp.einsum(
        "nqd,nkd->nqk", stacked, key_one, preferred_element_type=jnp.float32
    ) * factor
    if per_row:
        stacked_segment = jnp.repeat(row_segment, head_count, axis=1)
        stacked_index = jnp.repeat(row_index, head_count, axis=1)
        stacked_allowed = (stacked_segment[:, :, None] == key_segment[:, None, :]) & (
            key_index[:, None, :] <= stacked_index[:, :, None]
        )
        scores = jnp.where(stacked_allowed, scores, -1e30)
        peak = jnp.max(scores, axis=2, keepdims=True)
        weights = jnp.exp(scores - peak)
        weights = (weights / jnp.sum(weights, axis=2, keepdims=True)).astype(jnp.bfloat16)
    else:
        scores = scores.reshape(len(firsts), rows, head_count, span)
        scores = jnp.where(allowed[:, :, None, :], scores, -1e30)
        peak = jnp.max(scores, axis=3, keepdims=True)
        weights = jnp.exp(scores - peak)
        weights = (weights / jnp.sum(weights, axis=3, keepdims=True)).astype(jnp.bfloat16)
    attended = jnp.einsum(
        "nqk,nkd->nqd",
        weights.reshape(len(firsts), rows * head_count, span),
        value_one,
        preferred_element_type=jnp.float32,
    ).astype(jnp.bfloat16)
    if per_row:
        return attended.reshape(len(firsts), rows, head_count, HEAD_WIDTH)
    return attended.reshape(len(firsts), rows, head_count * HEAD_WIDTH)


def local(
    query_heads,
    normed_key_heads,
    value_rows_per_head,
    residual_in,
    out_weight,
    norm_gain,
    gate_up,
    down_weight,
    segment_ids,
    expert_ids,
    gate_weights,
):
    tok_rows = residual_in.shape[0]
    group_tokens = expert_ids.shape[0]
    size = lax.axis_size("tp")
    me = lax.axis_index("tp")
    token_positions = positions_of(segment_ids)
    keys_after_rotary = rotary_tables(
        normed_key_heads.reshape(group_tokens, 1, HEAD_WIDTH).astype(jnp.float32), token_positions
    ).astype(jnp.bfloat16)[:, 0]
    values = value_rows_per_head

    def projected_blocks(blocks, queries, per_row):
        attended = attend_blocks(
            queries, [block * tok_rows for block in blocks], tok_rows,
            keys_after_rotary, values, segment_ids, token_positions, per_row,
        )
        if per_row:
            return jnp.einsum(
                "nrhc,hcd->nrd", attended,
                out_weight.reshape(attended.shape[2], HEAD_WIDTH, -1),
                preferred_element_type=jnp.float32,
            )
        return jnp.einsum(
            "nrc,cd->nrd", attended, out_weight, preferred_element_type=jnp.float32
        )

    first_pair = projected_blocks([me ^ 3, me ^ 2], query_heads, True)
    partner_cross = lax.ppermute(first_pair[0].astype(jnp.bfloat16), "tp", xor_pairs(size, 1))
    across = (first_pair[1] + partner_cross.astype(jnp.float32)).astype(jnp.bfloat16)
    across, later_queries = lax.optimization_barrier((across, query_heads))
    from_across = lax.ppermute(across, "tp", xor_pairs(size, 2))
    second_pair = projected_blocks([me ^ 1, me], later_queries, False)
    partner_own = lax.ppermute(second_pair[0].astype(jnp.bfloat16), "tp", xor_pairs(size, 1))
    projected = (
        second_pair[1]
        + partner_own.astype(jnp.float32)
        + from_across.astype(jnp.float32)
    )
    mixed = (residual_in.astype(jnp.float32) + projected).astype(jnp.bfloat16)
    normed = rms_norm(mixed, norm_gain)

    capacity = min(group_tokens * expert_ids.shape[1] * 5 // (EXPERTS * 4), group_tokens)
    window = gate_up.shape[0]
    slots = jnp.arange(window, dtype=jnp.int32)
    hits = expert_ids[:, :, None] == slots[None, None, :]
    route_all = jnp.sum(jnp.where(hits, gate_weights[:, :, None], 0.0), axis=1)
    chosen = jnp.any(hits, axis=1)
    rank = jnp.cumsum(chosen.astype(jnp.int32), axis=0) - 1
    kk = jnp.arange(capacity, dtype=jnp.int32)
    select_all = (rank.T[:, None, :] == kk[None, :, None]) & chosen.T[:, None, :]
    route_sel = jnp.sum(jnp.where(select_all, route_all.T[:, None, :], 0.0), axis=-1)
    select_loc = lax.dynamic_slice_in_dim(select_all, me * tok_rows, tok_rows, axis=2)

    picked = jnp.einsum(
        "ekt,td->ekd", select_loc.astype(jnp.bfloat16), normed,
        preferred_element_type=jnp.float32,
    ).astype(jnp.bfloat16)
    picked = picked + lax.ppermute(picked, "tp", xor_pairs(size, 1))
    picked = picked + lax.ppermute(picked, "tp", xor_pairs(size, 2))
    gate = jnp.einsum("ekd,edf->ekf", picked, gate_up[:, 0], preferred_element_type=jnp.float32)
    upward = jnp.einsum("ekd,edf->ekf", picked, gate_up[:, 1], preferred_element_type=jnp.float32)
    active = (jax.nn.silu(gate) * upward).astype(jnp.bfloat16)
    outputs = jnp.einsum("ekf,efd->ekd", active, down_weight, preferred_element_type=jnp.float32)
    scaled = route_sel[:, :, None] * outputs
    scaled = scaled + lax.ppermute(scaled, "tp", xor_pairs(size, 1))
    scaled = scaled + lax.ppermute(
        scaled.astype(jnp.bfloat16), "tp", xor_pairs(size, 2)
    ).astype(jnp.float32)
    experts = jnp.einsum(
        "ekt,ekd->td", select_loc.astype(jnp.float32), scaled,
        precision=lax.Precision.HIGHEST, preferred_element_type=jnp.float32,
    )
    return (mixed.astype(jnp.float32) + experts).astype(jnp.bfloat16)


def solution(mesh):
    placed = (
        P("req", "tp"),
        P("req", "tp"),
        P("req", "tp"),
        P(("req", "tp"), None),
        P("tp", None),
        P(),
        P(None, None, None, "tp"),
        P(None, "tp", None),
        P("req"),
        P("req", None),
        P("req", None),
    )
    return jax.shard_map(
        local, mesh=mesh, in_specs=placed, out_specs=P(("req", "tp"), None), check_vma=False
    )
```

```python
import math

import jax
import jax.numpy as jnp
from jax import lax
from jax.sharding import PartitionSpec as P

QUERY_HEADS = 32
KEY_VALUE_HEADS = 4
HEAD_WIDTH = 128
EXPERTS = 128


def positions_of(segment_ids):
    earlier = (segment_ids[None, :] < segment_ids[:, None]).astype(jnp.int32)
    return jnp.arange(segment_ids.shape[0], dtype=jnp.int32) - jnp.sum(earlier, axis=1)


def rotary_tables(vectors, token_positions):
    half_dim = vectors.shape[-1] // 2
    frequency = 1000000.0 ** (-jnp.arange(half_dim, dtype=jnp.float32) / half_dim)
    angles = token_positions.astype(jnp.float32)[:, None] * frequency[None, :]
    cosine = jnp.cos(angles)[:, None, :]
    sine = jnp.sin(angles)[:, None, :]
    first = vectors[..., :half_dim]
    second = vectors[..., half_dim:]
    return jnp.concatenate(
        [first * cosine - second * sine, second * cosine + first * sine], axis=-1
    )


def rms_norm(hidden, gain):
    widened = hidden.astype(jnp.float32)
    factor = lax.rsqrt(jnp.mean(widened * widened, axis=-1, keepdims=True) + 1e-06)
    return (widened * factor * gain).astype(jnp.bfloat16)


SEG_MOST = 480


def xor_pairs(size, mask):
    return [(index, index ^ mask) for index in range(size)]


def attend_blocks(query_heads, firsts, rows, keys_after_rotary, values, segment_ids, token_positions):
    item_count = segment_ids.shape[0]
    span = min(item_count, rows + SEG_MOST)
    head_count = query_heads.shape[1] // HEAD_WIDTH
    starts = [jnp.clip(first + rows - span, 0, item_count - span) for first in firsts]
    row_index = jnp.stack([first + jnp.arange(rows, dtype=jnp.int32) for first in firsts])
    key_index = jnp.stack([start + jnp.arange(span, dtype=jnp.int32) for start in starts])
    row_segment = jnp.stack([lax.dynamic_slice_in_dim(segment_ids, f, rows) for f in firsts])
    key_segment = jnp.stack([lax.dynamic_slice_in_dim(segment_ids, s, span) for s in starts])
    allowed = (row_segment[:, :, None] == key_segment[:, None, :]) & (
        key_index[:, None, :] <= row_index[:, :, None]
    )
    key_one = jnp.stack([lax.dynamic_slice_in_dim(keys_after_rotary, s, span) for s in starts])
    value_one = jnp.stack([lax.dynamic_slice_in_dim(values, s, span) for s in starts])
    query_rows = jnp.concatenate([lax.dynamic_slice_in_dim(query_heads, f, rows) for f in firsts])
    row_positions = jnp.concatenate(
        [lax.dynamic_slice_in_dim(token_positions, f, rows) for f in firsts]
    )
    queries = rotary_tables(
        query_rows.reshape(len(firsts) * rows, head_count, HEAD_WIDTH).astype(jnp.float32),
        row_positions,
    ).astype(jnp.bfloat16)
    factor = 1.0 / math.sqrt(HEAD_WIDTH)
    stacked = queries.reshape(len(firsts), rows * head_count, HEAD_WIDTH)
    scores = jnp.einsum(
        "nqd,nkd->nqk", stacked, key_one, preferred_element_type=jnp.float32
    ) * factor
    scores = scores.reshape(len(firsts), rows, head_count, span)
    scores = jnp.where(allowed[:, :, None, :], scores, -1e30)
    peak = jnp.max(scores, axis=3, keepdims=True)
    weights = jnp.exp(scores - peak)
    weights = (weights / jnp.sum(weights, axis=3, keepdims=True)).astype(jnp.bfloat16)
    attended = jnp.einsum(
        "nqk,nkd->nqd",
        weights.reshape(len(firsts), rows * head_count, span),
        value_one,
        preferred_element_type=jnp.float32,
    ).astype(jnp.bfloat16)
    return attended.reshape(len(firsts), rows, head_count * HEAD_WIDTH)


def local(
    query_heads,
    normed_key_heads,
    value_rows_per_head,
    residual_in,
    out_weight,
    norm_gain,
    gate_up,
    down_weight,
    segment_ids,
    expert_ids,
    gate_weights,
):
    tok_rows = residual_in.shape[0]
    group_tokens = expert_ids.shape[0]
    size = lax.axis_size("tp")
    me = lax.axis_index("tp")
    token_positions = positions_of(segment_ids)
    keys_after_rotary = rotary_tables(
        normed_key_heads.reshape(group_tokens, 1, HEAD_WIDTH).astype(jnp.float32), token_positions
    ).astype(jnp.bfloat16)[:, 0]
    values = value_rows_per_head

    def projected_blocks(blocks, queries):
        attended = attend_blocks(
            queries, [block * tok_rows for block in blocks], tok_rows,
            keys_after_rotary, values, segment_ids, token_positions,
        )
        return jnp.einsum(
            "nrc,cd->nrd", attended, out_weight, preferred_element_type=jnp.float32
        )

    first_pair = projected_blocks([me ^ 3, me ^ 2], query_heads)
    partner_cross = lax.ppermute(first_pair[0].astype(jnp.bfloat16), "tp", xor_pairs(size, 1))
    across = (first_pair[1] + partner_cross.astype(jnp.float32)).astype(jnp.bfloat16)
    across, later_queries = lax.optimization_barrier((across, query_heads))
    from_across = lax.ppermute(across, "tp", xor_pairs(size, 2))
    second_pair = projected_blocks([me ^ 1, me], later_queries)
    partner_own = lax.ppermute(second_pair[0].astype(jnp.bfloat16), "tp", xor_pairs(size, 1))
    projected = (
        second_pair[1]
        + partner_own.astype(jnp.float32)
        + from_across.astype(jnp.float32)
    )
    mixed = (residual_in.astype(jnp.float32) + projected).astype(jnp.bfloat16)
    normed = rms_norm(mixed, norm_gain)

    capacity = min(group_tokens * expert_ids.shape[1] * 5 // (EXPERTS * 4), group_tokens)
    window = gate_up.shape[0]
    slots = jnp.arange(window, dtype=jnp.int32)
    hits = expert_ids[:, :, None] == slots[None, None, :]
    route_all = jnp.sum(jnp.where(hits, gate_weights[:, :, None], 0.0), axis=1)
    chosen = jnp.any(hits, axis=1)
    rank = jnp.cumsum(chosen.astype(jnp.int32), axis=0) - 1
    kk = jnp.arange(-(-capacity // 8) * 8, dtype=jnp.int32)
    select_all = (rank.T[:, None, :] == kk[None, :, None]) & chosen.T[:, None, :]
    route_sel = jnp.sum(jnp.where(select_all, route_all.T[:, None, :], 0.0), axis=-1)
    select_loc = lax.dynamic_slice_in_dim(select_all, me * tok_rows, tok_rows, axis=2)

    picked = jnp.einsum(
        "ekt,td->ekd", select_loc.astype(jnp.bfloat16), normed,
        preferred_element_type=jnp.float32,
    ).astype(jnp.bfloat16)
    picked = picked + lax.ppermute(picked, "tp", xor_pairs(size, 1))
    picked = picked + lax.ppermute(picked, "tp", xor_pairs(size, 2))
    gate = jnp.einsum("ekd,edf->ekf", picked, gate_up[:, 0], preferred_element_type=jnp.float32)
    upward = jnp.einsum("ekd,edf->ekf", picked, gate_up[:, 1], preferred_element_type=jnp.float32)
    active = (jax.nn.silu(gate) * upward).astype(jnp.bfloat16)
    outputs = jnp.einsum("ekf,efd->ekd", active, down_weight, preferred_element_type=jnp.float32)
    scaled = route_sel[:, :, None] * outputs
    scaled = scaled + lax.ppermute(scaled, "tp", xor_pairs(size, 1))
    scaled = scaled + lax.ppermute(
        scaled.astype(jnp.bfloat16), "tp", xor_pairs(size, 2)
    ).astype(jnp.float32)
    experts = jnp.einsum(
        "ekt,ekd->td", select_loc.astype(jnp.float32), scaled,
        precision=lax.Precision.HIGHEST, preferred_element_type=jnp.float32,
    )
    return (mixed.astype(jnp.float32) + experts).astype(jnp.bfloat16)


def solution(mesh):
    placed = (
        P("req", "tp"),
        P("req", "tp"),
        P("req", "tp"),
        P(("req", "tp"), None),
        P("tp", None),
        P(),
        P(None, None, None, "tp"),
        P(None, "tp", None),
        P("req"),
        P("req", None),
        P("req", None),
    )
    return jax.shard_map(
        local, mesh=mesh, in_specs=placed, out_specs=P(("req", "tp"), None), check_vma=False
    )
```

```python
import math

import jax
import jax.numpy as jnp
from jax import lax
from jax.sharding import PartitionSpec as P

QUERY_HEADS = 32
KEY_VALUE_HEADS = 4
HEAD_WIDTH = 128
EXPERTS = 128


def positions_of(segment_ids):
    earlier = (segment_ids[None, :] < segment_ids[:, None]).astype(jnp.int32)
    return jnp.arange(segment_ids.shape[0], dtype=jnp.int32) - jnp.sum(earlier, axis=1)


def rotary_tables(vectors, token_positions):
    half_dim = vectors.shape[-1] // 2
    frequency = 1000000.0 ** (-jnp.arange(half_dim, dtype=jnp.float32) / half_dim)
    angles = token_positions.astype(jnp.float32)[:, None] * frequency[None, :]
    cosine = jnp.cos(angles)[:, None, :]
    sine = jnp.sin(angles)[:, None, :]
    first = vectors[..., :half_dim]
    second = vectors[..., half_dim:]
    return jnp.concatenate(
        [first * cosine - second * sine, second * cosine + first * sine], axis=-1
    )


def rms_norm(hidden, gain):
    widened = hidden.astype(jnp.float32)
    factor = lax.rsqrt(jnp.mean(widened * widened, axis=-1, keepdims=True) + 1e-06)
    return (widened * factor * gain).astype(jnp.bfloat16)


SEG_MOST = 480


def xor_pairs(size, mask):
    return [(index, index ^ mask) for index in range(size)]


def attend_blocks(query_heads, firsts, rows, keys_after_rotary, values, segment_ids, token_positions):
    item_count = segment_ids.shape[0]
    span = min(item_count, rows + SEG_MOST)
    head_count = query_heads.shape[1] // HEAD_WIDTH
    starts = [jnp.clip(first + rows - span, 0, item_count - span) for first in firsts]
    row_index = jnp.stack([first + jnp.arange(rows, dtype=jnp.int32) for first in firsts])
    key_index = jnp.stack([start + jnp.arange(span, dtype=jnp.int32) for start in starts])
    row_segment = jnp.stack([lax.dynamic_slice_in_dim(segment_ids, f, rows) for f in firsts])
    key_segment = jnp.stack([lax.dynamic_slice_in_dim(segment_ids, s, span) for s in starts])
    allowed = (row_segment[:, :, None] == key_segment[:, None, :]) & (
        key_index[:, None, :] <= row_index[:, :, None]
    )
    key_one = jnp.stack([lax.dynamic_slice_in_dim(keys_after_rotary, s, span) for s in starts])
    value_one = jnp.stack([lax.dynamic_slice_in_dim(values, s, span) for s in starts])
    query_rows = jnp.concatenate([lax.dynamic_slice_in_dim(query_heads, f, rows) for f in firsts])
    row_positions = jnp.concatenate(
        [lax.dynamic_slice_in_dim(token_positions, f, rows) for f in firsts]
    )
    queries = rotary_tables(
        query_rows.reshape(len(firsts) * rows, head_count, HEAD_WIDTH).astype(jnp.float32),
        row_positions,
    ).astype(jnp.bfloat16)
    factor = 1.0 / math.sqrt(HEAD_WIDTH)
    stacked = queries.reshape(len(firsts), rows * head_count, HEAD_WIDTH)
    scores = jnp.einsum(
        "nqd,nkd->nqk", stacked, key_one, preferred_element_type=jnp.float32
    ) * factor
    scores = scores.reshape(len(firsts), rows, head_count, span)
    scores = jnp.where(allowed[:, :, None, :], scores, -1e30)
    peak = jnp.max(scores, axis=3, keepdims=True)
    weights = jnp.exp(scores - peak)
    weights = (weights / jnp.sum(weights, axis=3, keepdims=True)).astype(jnp.bfloat16)
    attended = jnp.einsum(
        "nqk,nkd->nqd",
        weights.reshape(len(firsts), rows * head_count, span),
        value_one,
        preferred_element_type=jnp.float32,
    ).astype(jnp.bfloat16)
    return attended.reshape(len(firsts), rows, head_count, HEAD_WIDTH)


def local(
    query_heads,
    normed_key_heads,
    value_rows_per_head,
    residual_in,
    out_weight,
    norm_gain,
    gate_up,
    down_weight,
    segment_ids,
    expert_ids,
    gate_weights,
):
    tok_rows = residual_in.shape[0]
    group_tokens = expert_ids.shape[0]
    size = lax.axis_size("tp")
    me = lax.axis_index("tp")
    token_positions = positions_of(segment_ids)
    keys_after_rotary = rotary_tables(
        normed_key_heads.reshape(group_tokens, 1, HEAD_WIDTH).astype(jnp.float32), token_positions
    ).astype(jnp.bfloat16)[:, 0]
    values = value_rows_per_head

    def projected_blocks(blocks, queries):
        attended = attend_blocks(
            queries, [block * tok_rows for block in blocks], tok_rows,
            keys_after_rotary, values, segment_ids, token_positions,
        )
        return jnp.einsum(
            "nrhc,hcd->nrd", attended, out_weight.reshape(attended.shape[2], HEAD_WIDTH, -1),
            preferred_element_type=jnp.float32,
        )

    first_pair = projected_blocks([me ^ 3, me ^ 2], query_heads)
    partner_cross = lax.ppermute(first_pair[0].astype(jnp.bfloat16), "tp", xor_pairs(size, 1))
    across = (first_pair[1] + partner_cross.astype(jnp.float32)).astype(jnp.bfloat16)
    across, later_queries = lax.optimization_barrier((across, query_heads))
    from_across = lax.ppermute(across, "tp", xor_pairs(size, 2))
    second_pair = projected_blocks([me ^ 1, me], later_queries)
    partner_own = lax.ppermute(second_pair[0].astype(jnp.bfloat16), "tp", xor_pairs(size, 1))
    projected = (
        second_pair[1]
        + partner_own.astype(jnp.float32)
        + from_across.astype(jnp.float32)
    )
    mixed = (residual_in.astype(jnp.float32) + projected).astype(jnp.bfloat16)
    normed = rms_norm(mixed, norm_gain)

    capacity = min(group_tokens * expert_ids.shape[1] * 5 // (EXPERTS * 4), group_tokens)
    window = gate_up.shape[0]
    slots = jnp.arange(window, dtype=jnp.int32)
    hits = expert_ids[:, :, None] == slots[None, None, :]
    route_all = jnp.sum(jnp.where(hits, gate_weights[:, :, None], 0.0), axis=1)
    chosen = jnp.any(hits, axis=1)
    rank = jnp.cumsum(chosen.astype(jnp.int32), axis=0) - 1
    kk = jnp.arange(-(-capacity // 8) * 8, dtype=jnp.int32)
    select_all = (rank.T[:, None, :] == kk[None, :, None]) & chosen.T[:, None, :]
    route_sel = jnp.sum(jnp.where(select_all, route_all.T[:, None, :], 0.0), axis=-1)
    select_loc = lax.dynamic_slice_in_dim(select_all, me * tok_rows, tok_rows, axis=2)

    picked = jnp.einsum(
        "ekt,td->ekd", select_loc.astype(jnp.bfloat16), normed,
        preferred_element_type=jnp.float32,
    ).astype(jnp.bfloat16)
    picked = picked + lax.ppermute(picked, "tp", xor_pairs(size, 1))
    picked = picked + lax.ppermute(picked, "tp", xor_pairs(size, 2))
    gate = jnp.einsum("ekd,edf->ekf", picked, gate_up[:, 0], preferred_element_type=jnp.float32)
    upward = jnp.einsum("ekd,edf->ekf", picked, gate_up[:, 1], preferred_element_type=jnp.float32)
    active = (jax.nn.silu(gate) * upward).astype(jnp.bfloat16)
    outputs = jnp.einsum("ekf,efd->ekd", active, down_weight, preferred_element_type=jnp.float32)
    scaled = route_sel[:, :, None] * outputs
    scaled = scaled + lax.ppermute(scaled, "tp", xor_pairs(size, 1))
    scaled = scaled + lax.ppermute(
        scaled.astype(jnp.bfloat16), "tp", xor_pairs(size, 2)
    ).astype(jnp.float32)
    experts = jnp.einsum(
        "ekt,ekd->td", select_loc.astype(jnp.float32), scaled,
        precision=lax.Precision.HIGHEST, preferred_element_type=jnp.float32,
    )
    return (mixed.astype(jnp.float32) + experts).astype(jnp.bfloat16)


def solution(mesh):
    placed = (
        P("req", "tp"),
        P("req", "tp"),
        P("req", "tp"),
        P(("req", "tp"), None),
        P("tp", None),
        P(),
        P(None, None, None, "tp"),
        P(None, "tp", None),
        P("req"),
        P("req", None),
        P("req", None),
    )
    return jax.shard_map(
        local, mesh=mesh, in_specs=placed, out_specs=P(("req", "tp"), None), check_vma=False
    )
```

```python
import math

import jax
import jax.numpy as jnp
from jax import lax
from jax.sharding import PartitionSpec as P

QUERY_HEADS = 32
KEY_VALUE_HEADS = 4
HEAD_WIDTH = 128
EXPERTS = 128


def positions_of(segment_ids):
    earlier = (segment_ids[None, :] < segment_ids[:, None]).astype(jnp.int32)
    return jnp.arange(segment_ids.shape[0], dtype=jnp.int32) - jnp.sum(earlier, axis=1)


def rotary_tables(vectors, token_positions):
    half_dim = vectors.shape[-1] // 2
    frequency = 1000000.0 ** (-jnp.arange(half_dim, dtype=jnp.float32) / half_dim)
    angles = token_positions.astype(jnp.float32)[:, None] * frequency[None, :]
    cosine = jnp.cos(angles)[:, None, :]
    sine = jnp.sin(angles)[:, None, :]
    first = vectors[..., :half_dim]
    second = vectors[..., half_dim:]
    return jnp.concatenate(
        [first * cosine - second * sine, second * cosine + first * sine], axis=-1
    )


def rms_norm(hidden, gain):
    widened = hidden.astype(jnp.float32)
    factor = lax.rsqrt(jnp.mean(widened * widened, axis=-1, keepdims=True) + 1e-06)
    return (widened * factor * gain).astype(jnp.bfloat16)


SEG_MOST = 480


def xor_pairs(size, mask):
    return [(index, index ^ mask) for index in range(size)]


def attend_blocks(query_heads, firsts, rows, keys_after_rotary, values, segment_ids, token_positions):
    item_count = segment_ids.shape[0]
    span = min(item_count, rows + SEG_MOST)
    head_count = query_heads.shape[1] // HEAD_WIDTH
    starts = [jnp.clip(first + rows - span, 0, item_count - span) for first in firsts]
    row_index = jnp.stack([first + jnp.arange(rows, dtype=jnp.int32) for first in firsts])
    key_index = jnp.stack([start + jnp.arange(span, dtype=jnp.int32) for start in starts])
    row_segment = jnp.stack([lax.dynamic_slice_in_dim(segment_ids, f, rows) for f in firsts])
    key_segment = jnp.stack([lax.dynamic_slice_in_dim(segment_ids, s, span) for s in starts])
    key_one = jnp.stack([lax.dynamic_slice_in_dim(keys_after_rotary, s, span) for s in starts])
    value_one = jnp.stack([lax.dynamic_slice_in_dim(values, s, span) for s in starts])
    query_rows = jnp.concatenate([lax.dynamic_slice_in_dim(query_heads, f, rows) for f in firsts])
    row_positions = jnp.concatenate(
        [lax.dynamic_slice_in_dim(token_positions, f, rows) for f in firsts]
    )
    queries = rotary_tables(
        query_rows.reshape(len(firsts) * rows, head_count, HEAD_WIDTH).astype(jnp.float32),
        row_positions,
    ).astype(jnp.bfloat16)
    factor = 1.0 / math.sqrt(HEAD_WIDTH)
    stacked = queries.reshape(len(firsts), rows * head_count, HEAD_WIDTH)
    scores = jnp.einsum(
        "nqd,nkd->nqk", stacked, key_one, preferred_element_type=jnp.float32
    ) * factor
    stacked_segment = jnp.repeat(row_segment, head_count, axis=1)
    stacked_index = jnp.repeat(row_index, head_count, axis=1)
    allowed = (stacked_segment[:, :, None] == key_segment[:, None, :]) & (
        key_index[:, None, :] <= stacked_index[:, :, None]
    )
    scores = jnp.where(allowed, scores, -1e30)
    peak = jnp.max(scores, axis=2, keepdims=True)
    weights = jnp.exp(scores - peak)
    weights = (weights / jnp.sum(weights, axis=2, keepdims=True)).astype(jnp.bfloat16)
    attended = jnp.einsum(
        "nqk,nkd->nqd",
        weights,
        value_one,
        preferred_element_type=jnp.float32,
    ).astype(jnp.bfloat16)
    return attended.reshape(len(firsts), rows, head_count, HEAD_WIDTH)


def local(
    query_heads,
    normed_key_heads,
    value_rows_per_head,
    residual_in,
    out_weight,
    norm_gain,
    gate_up,
    down_weight,
    segment_ids,
    expert_ids,
    gate_weights,
):
    tok_rows = residual_in.shape[0]
    group_tokens = expert_ids.shape[0]
    size = lax.axis_size("tp")
    me = lax.axis_index("tp")
    token_positions = positions_of(segment_ids)
    keys_after_rotary = rotary_tables(
        normed_key_heads.reshape(group_tokens, 1, HEAD_WIDTH).astype(jnp.float32), token_positions
    ).astype(jnp.bfloat16)[:, 0]
    values = value_rows_per_head

    def projected_blocks(blocks, queries):
        attended = attend_blocks(
            queries, [block * tok_rows for block in blocks], tok_rows,
            keys_after_rotary, values, segment_ids, token_positions,
        )
        return jnp.einsum(
            "nrhc,hcd->nrd", attended, out_weight.reshape(attended.shape[2], HEAD_WIDTH, -1),
            preferred_element_type=jnp.float32,
        )

    first_pair = projected_blocks([me ^ 3, me ^ 2], query_heads)
    partner_cross = lax.ppermute(first_pair[0].astype(jnp.bfloat16), "tp", xor_pairs(size, 1))
    across = first_pair[1] + partner_cross.astype(jnp.float32)
    across, later_queries = lax.optimization_barrier((across, query_heads))
    from_across = lax.ppermute(across, "tp", xor_pairs(size, 2))
    second_pair = projected_blocks([me ^ 1, me], later_queries)
    partner_own = lax.ppermute(second_pair[0].astype(jnp.bfloat16), "tp", xor_pairs(size, 1))
    projected = (
        second_pair[1]
        + partner_own.astype(jnp.float32)
        + from_across.astype(jnp.float32)
    )
    mixed = (residual_in.astype(jnp.float32) + projected).astype(jnp.bfloat16)
    normed = rms_norm(mixed, norm_gain)

    capacity = min(group_tokens * expert_ids.shape[1] * 5 // (EXPERTS * 4), group_tokens)
    window = gate_up.shape[0]
    slots = jnp.arange(window, dtype=jnp.int32)
    hits = expert_ids[:, :, None] == slots[None, None, :]
    route_all = jnp.sum(jnp.where(hits, gate_weights[:, :, None], 0.0), axis=1)
    chosen = jnp.any(hits, axis=1)
    rank = jnp.cumsum(chosen.astype(jnp.int32), axis=0) - 1
    kk = jnp.arange(-(-capacity // 8) * 8, dtype=jnp.int32)
    select_all = (rank.T[:, None, :] == kk[None, :, None]) & chosen.T[:, None, :]
    route_sel = jnp.sum(jnp.where(select_all, route_all.T[:, None, :], 0.0), axis=-1)
    select_loc = lax.dynamic_slice_in_dim(select_all, me * tok_rows, tok_rows, axis=2)

    picked = jnp.einsum(
        "ekt,td->ekd", select_loc.astype(jnp.bfloat16), normed,
        preferred_element_type=jnp.float32,
    ).astype(jnp.bfloat16)
    picked = picked + lax.ppermute(picked, "tp", xor_pairs(size, 1))
    picked = picked + lax.ppermute(picked, "tp", xor_pairs(size, 2))
    gate = jnp.einsum("ekd,edf->ekf", picked, gate_up[:, 0], preferred_element_type=jnp.float32)
    upward = jnp.einsum("ekd,edf->ekf", picked, gate_up[:, 1], preferred_element_type=jnp.float32)
    active = (jax.nn.silu(gate) * upward).astype(jnp.bfloat16)
    outputs = jnp.einsum("ekf,efd->ekd", active, down_weight, preferred_element_type=jnp.float32)
    scaled = route_sel[:, :, None] * outputs
    scaled = scaled + lax.ppermute(scaled, "tp", xor_pairs(size, 1))
    scaled = scaled + lax.ppermute(
        scaled.astype(jnp.bfloat16), "tp", xor_pairs(size, 2)
    ).astype(jnp.float32)
    experts = jnp.einsum(
        "ekt,ekd->td", select_loc.astype(jnp.float32), scaled,
        precision=lax.Precision.HIGHEST, preferred_element_type=jnp.float32,
    )
    return (mixed.astype(jnp.float32) + experts).astype(jnp.bfloat16)


def solution(mesh):
    placed = (
        P("req", "tp"),
        P("req", "tp"),
        P("req", "tp"),
        P(("req", "tp"), None),
        P("tp", None),
        P(),
        P(None, None, None, "tp"),
        P(None, "tp", None),
        P("req"),
        P("req", None),
        P("req", None),
    )
    return jax.shard_map(
        local, mesh=mesh, in_specs=placed, out_specs=P(("req", "tp"), None), check_vma=False
    )
```

```python
import math

import jax
import jax.numpy as jnp
from jax import lax
from jax.sharding import PartitionSpec as P

QUERY_HEADS = 32
KEY_VALUE_HEADS = 4
HEAD_WIDTH = 128
EXPERTS = 128


def positions_of(segment_ids):
    earlier = (segment_ids[None, :] < segment_ids[:, None]).astype(jnp.int32)
    return jnp.arange(segment_ids.shape[0], dtype=jnp.int32) - jnp.sum(earlier, axis=1)


def rotary_tables(vectors, token_positions):
    half_dim = vectors.shape[-1] // 2
    frequency = 1000000.0 ** (-jnp.arange(half_dim, dtype=jnp.float32) / half_dim)
    angles = token_positions.astype(jnp.float32)[:, None] * frequency[None, :]
    cosine = jnp.cos(angles)[:, None, :]
    sine = jnp.sin(angles)[:, None, :]
    first = vectors[..., :half_dim]
    second = vectors[..., half_dim:]
    return jnp.concatenate(
        [first * cosine - second * sine, second * cosine + first * sine], axis=-1
    )


def rms_norm(hidden, gain):
    widened = hidden.astype(jnp.float32)
    factor = lax.rsqrt(jnp.mean(widened * widened, axis=-1, keepdims=True) + 1e-06)
    return (widened * factor * gain).astype(jnp.bfloat16)


SEG_MOST = 480


def xor_pairs(size, mask):
    return [(index, index ^ mask) for index in range(size)]


def attend_blocks(query_heads, firsts, rows, keys_after_rotary, values, segment_ids, token_positions):
    item_count = segment_ids.shape[0]
    span = min(item_count, rows + SEG_MOST)
    head_count = query_heads.shape[1] // HEAD_WIDTH
    starts = [jnp.clip(first + rows - span, 0, item_count - span) for first in firsts]
    row_index = jnp.stack([first + jnp.arange(rows, dtype=jnp.int32) for first in firsts])
    key_index = jnp.stack([start + jnp.arange(span, dtype=jnp.int32) for start in starts])
    row_segment = jnp.stack([lax.dynamic_slice_in_dim(segment_ids, f, rows) for f in firsts])
    key_segment = jnp.stack([lax.dynamic_slice_in_dim(segment_ids, s, span) for s in starts])
    key_one = jnp.stack([lax.dynamic_slice_in_dim(keys_after_rotary, s, span) for s in starts])
    value_one = jnp.stack([lax.dynamic_slice_in_dim(values, s, span) for s in starts])
    query_rows = jnp.concatenate([lax.dynamic_slice_in_dim(query_heads, f, rows) for f in firsts])
    row_positions = jnp.concatenate(
        [lax.dynamic_slice_in_dim(token_positions, f, rows) for f in firsts]
    )
    queries = rotary_tables(
        query_rows.reshape(len(firsts) * rows, head_count, HEAD_WIDTH).astype(jnp.float32),
        row_positions,
    ).astype(jnp.bfloat16)
    factor = 1.0 / math.sqrt(HEAD_WIDTH)
    stacked = queries.reshape(len(firsts), rows * head_count, HEAD_WIDTH)
    scores = jnp.einsum(
        "nqd,nkd->nqk", stacked, key_one, preferred_element_type=jnp.float32
    ) * factor
    stacked_segment = jnp.repeat(row_segment, head_count, axis=1)
    stacked_index = jnp.repeat(row_index, head_count, axis=1)
    allowed = (stacked_segment[:, :, None] == key_segment[:, None, :]) & (
        key_index[:, None, :] <= stacked_index[:, :, None]
    )
    scores = jnp.where(allowed, scores, -1e30)
    peak = jnp.max(scores, axis=2, keepdims=True)
    weights = jnp.exp(scores - peak)
    weights = (weights / jnp.sum(weights, axis=2, keepdims=True)).astype(jnp.bfloat16)
    attended = jnp.einsum(
        "nqk,nkd->nqd",
        weights,
        value_one,
        preferred_element_type=jnp.float32,
    ).astype(jnp.bfloat16)
    return attended.reshape(len(firsts), rows, head_count, HEAD_WIDTH)


def local(
    query_heads,
    normed_key_heads,
    value_rows_per_head,
    residual_in,
    out_weight,
    norm_gain,
    gate_up,
    down_weight,
    segment_ids,
    expert_ids,
    gate_weights,
):
    tok_rows = residual_in.shape[0]
    group_tokens = expert_ids.shape[0]
    size = lax.axis_size("tp")
    me = lax.axis_index("tp")
    token_positions = positions_of(segment_ids)
    keys_after_rotary = rotary_tables(
        normed_key_heads.reshape(group_tokens, 1, HEAD_WIDTH).astype(jnp.float32), token_positions
    ).astype(jnp.bfloat16)[:, 0]
    values = value_rows_per_head

    def projected_blocks(blocks, queries):
        attended = attend_blocks(
            queries, [block * tok_rows for block in blocks], tok_rows,
            keys_after_rotary, values, segment_ids, token_positions,
        )
        return jnp.einsum(
            "nrhc,hcd->nrd", attended, out_weight.reshape(attended.shape[2], HEAD_WIDTH, -1),
            preferred_element_type=jnp.float32,
        )

    first_pair = projected_blocks([me ^ 3, me ^ 2], query_heads)
    partner_cross = lax.ppermute(first_pair[0].astype(jnp.bfloat16), "tp", xor_pairs(size, 1))
    across = first_pair[1] + partner_cross.astype(jnp.float32)
    high = across.astype(jnp.bfloat16)
    half = across.shape[1] // 2
    low = (across[:, :half] - high[:, :half].astype(jnp.float32)).astype(jnp.bfloat16)
    message, later_queries = lax.optimization_barrier(
        (jnp.concatenate([high, low], axis=1), query_heads)
    )
    message = lax.ppermute(message, "tp", xor_pairs(size, 2)).astype(jnp.float32)
    from_across = message[:, : 2 * half] + jnp.pad(message[:, 2 * half :], ((0, 0), (0, half)))
    second_pair = projected_blocks([me ^ 1, me], later_queries)
    partner_own = lax.ppermute(second_pair[0].astype(jnp.bfloat16), "tp", xor_pairs(size, 1))
    projected = (
        second_pair[1]
        + partner_own.astype(jnp.float32)
        + from_across.astype(jnp.float32)
    )
    mixed = (residual_in.astype(jnp.float32) + projected).astype(jnp.bfloat16)
    normed = rms_norm(mixed, norm_gain)

    capacity = min(group_tokens * expert_ids.shape[1] * 5 // (EXPERTS * 4), group_tokens)
    window = gate_up.shape[0]
    slots = jnp.arange(window, dtype=jnp.int32)
    hits = expert_ids[:, :, None] == slots[None, None, :]
    route_all = jnp.sum(jnp.where(hits, gate_weights[:, :, None], 0.0), axis=1)
    chosen = jnp.any(hits, axis=1)
    rank = jnp.cumsum(chosen.astype(jnp.int32), axis=0) - 1
    kk = jnp.arange(-(-capacity // 8) * 8, dtype=jnp.int32)
    select_all = (rank.T[:, None, :] == kk[None, :, None]) & chosen.T[:, None, :]
    route_sel = jnp.sum(jnp.where(select_all, route_all.T[:, None, :], 0.0), axis=-1)
    select_loc = lax.dynamic_slice_in_dim(select_all, me * tok_rows, tok_rows, axis=2)

    picked = jnp.einsum(
        "ekt,td->ekd", select_loc.astype(jnp.bfloat16), normed,
        preferred_element_type=jnp.float32,
    ).astype(jnp.bfloat16)
    picked = picked + lax.ppermute(picked, "tp", xor_pairs(size, 1))
    picked = picked + lax.ppermute(picked, "tp", xor_pairs(size, 2))
    gate = jnp.einsum("ekd,edf->ekf", picked, gate_up[:, 0], preferred_element_type=jnp.float32)
    upward = jnp.einsum("ekd,edf->ekf", picked, gate_up[:, 1], preferred_element_type=jnp.float32)
    active = (jax.nn.silu(gate) * upward).astype(jnp.bfloat16)
    outputs = jnp.einsum("ekf,efd->ekd", active, down_weight, preferred_element_type=jnp.float32)
    scaled = route_sel[:, :, None] * outputs
    scaled = scaled + lax.ppermute(scaled, "tp", xor_pairs(size, 1))
    scaled = scaled + lax.ppermute(
        scaled.astype(jnp.bfloat16), "tp", xor_pairs(size, 2)
    ).astype(jnp.float32)
    experts = jnp.einsum(
        "ekt,ekd->td", select_loc.astype(jnp.float32), scaled,
        precision=lax.Precision.HIGHEST, preferred_element_type=jnp.float32,
    )
    return (mixed.astype(jnp.float32) + experts).astype(jnp.bfloat16)


def solution(mesh):
    placed = (
        P("req", "tp"),
        P("req", "tp"),
        P("req", "tp"),
        P(("req", "tp"), None),
        P("tp", None),
        P(),
        P(None, None, None, "tp"),
        P(None, "tp", None),
        P("req"),
        P("req", None),
        P("req", None),
    )
    return jax.shard_map(
        local, mesh=mesh, in_specs=placed, out_specs=P(("req", "tp"), None), check_vma=False
    )
```

```python
import math

import jax
import jax.numpy as jnp
from jax import lax
from jax.sharding import PartitionSpec as P

QUERY_HEADS = 32
KEY_VALUE_HEADS = 4
HEAD_WIDTH = 128
EXPERTS = 128


def positions_of(segment_ids):
    earlier = (segment_ids[None, :] < segment_ids[:, None]).astype(jnp.int32)
    return jnp.arange(segment_ids.shape[0], dtype=jnp.int32) - jnp.sum(earlier, axis=1)


def rotary_tables(vectors, token_positions):
    half_dim = vectors.shape[-1] // 2
    frequency = 1000000.0 ** (-jnp.arange(half_dim, dtype=jnp.float32) / half_dim)
    angles = token_positions.astype(jnp.float32)[:, None] * frequency[None, :]
    cosine = jnp.cos(angles)[:, None, :]
    sine = jnp.sin(angles)[:, None, :]
    first = vectors[..., :half_dim]
    second = vectors[..., half_dim:]
    return jnp.concatenate(
        [first * cosine - second * sine, second * cosine + first * sine], axis=-1
    )


def rms_norm(hidden, gain):
    widened = hidden.astype(jnp.float32)
    factor = lax.rsqrt(jnp.mean(widened * widened, axis=-1, keepdims=True) + 1e-06)
    return (widened * factor * gain).astype(jnp.bfloat16)


SEG_MOST = 480


def xor_pairs(size, mask):
    return [(index, index ^ mask) for index in range(size)]


def attend_blocks(query_heads, firsts, rows, keys_after_rotary, values, segment_ids, token_positions):
    item_count = segment_ids.shape[0]
    span = min(item_count, rows + SEG_MOST)
    head_count = query_heads.shape[1] // HEAD_WIDTH
    starts = [jnp.clip(first + rows - span, 0, item_count - span) for first in firsts]
    row_index = jnp.stack([first + jnp.arange(rows, dtype=jnp.int32) for first in firsts])
    key_index = jnp.stack([start + jnp.arange(span, dtype=jnp.int32) for start in starts])
    row_segment = jnp.stack([lax.dynamic_slice_in_dim(segment_ids, f, rows) for f in firsts])
    key_segment = jnp.stack([lax.dynamic_slice_in_dim(segment_ids, s, span) for s in starts])
    key_one = jnp.stack([lax.dynamic_slice_in_dim(keys_after_rotary, s, span) for s in starts])
    value_one = jnp.stack([lax.dynamic_slice_in_dim(values, s, span) for s in starts])
    query_rows = jnp.concatenate([lax.dynamic_slice_in_dim(query_heads, f, rows) for f in firsts])
    row_positions = jnp.concatenate(
        [lax.dynamic_slice_in_dim(token_positions, f, rows) for f in firsts]
    )
    queries = rotary_tables(
        query_rows.reshape(len(firsts) * rows, head_count, HEAD_WIDTH).astype(jnp.float32),
        row_positions,
    ).astype(jnp.bfloat16)
    factor = 1.0 / math.sqrt(HEAD_WIDTH)
    stacked = queries.reshape(len(firsts), rows * head_count, HEAD_WIDTH)
    scores = jnp.einsum(
        "nqd,nkd->nqk", stacked, key_one, preferred_element_type=jnp.float32
    ) * factor
    stacked_segment = jnp.repeat(row_segment, head_count, axis=1)
    stacked_index = jnp.repeat(row_index, head_count, axis=1)
    allowed = (stacked_segment[:, :, None] == key_segment[:, None, :]) & (
        key_index[:, None, :] <= stacked_index[:, :, None]
    )
    scores = jnp.where(allowed, scores, -1e30)
    peak = jnp.max(scores, axis=2, keepdims=True)
    weights = jnp.exp(scores - peak)
    weights = (weights / jnp.sum(weights, axis=2, keepdims=True)).astype(jnp.bfloat16)
    attended = jnp.einsum(
        "nqk,nkd->nqd",
        weights,
        value_one,
        preferred_element_type=jnp.float32,
    ).astype(jnp.bfloat16)
    return attended.reshape(len(firsts), rows, head_count, HEAD_WIDTH)


def local(
    query_heads,
    normed_key_heads,
    value_rows_per_head,
    residual_in,
    out_weight,
    norm_gain,
    gate_up,
    down_weight,
    segment_ids,
    expert_ids,
    gate_weights,
):
    tok_rows = residual_in.shape[0]
    group_tokens = expert_ids.shape[0]
    size = lax.axis_size("tp")
    me = lax.axis_index("tp")
    token_positions = positions_of(segment_ids)
    keys_after_rotary = rotary_tables(
        normed_key_heads.reshape(group_tokens, 1, HEAD_WIDTH).astype(jnp.float32), token_positions
    ).astype(jnp.bfloat16)[:, 0]
    values = value_rows_per_head

    def projected_blocks(blocks, queries):
        attended = attend_blocks(
            queries, [block * tok_rows for block in blocks], tok_rows,
            keys_after_rotary, values, segment_ids, token_positions,
        )
        return jnp.einsum(
            "nrhc,hcd->nrd", attended, out_weight.reshape(attended.shape[2], HEAD_WIDTH, -1),
            preferred_element_type=jnp.float32,
        )

    first_pair = projected_blocks([me ^ 3, me ^ 2], query_heads)
    partner_cross = lax.ppermute(first_pair[0].astype(jnp.bfloat16), "tp", xor_pairs(size, 1))
    across = first_pair[1] + partner_cross.astype(jnp.float32)
    high = across.astype(jnp.bfloat16)
    half = across.shape[1] // 2
    low = (across[:, :half] - high[:, :half].astype(jnp.float32)).astype(jnp.bfloat16)
    message, later_queries = lax.optimization_barrier(
        (jnp.concatenate([high, low], axis=1), query_heads)
    )
    message = lax.ppermute(message, "tp", xor_pairs(size, 2)).astype(jnp.float32)
    from_across = message[:, : 2 * half] + jnp.pad(message[:, 2 * half :], ((0, 0), (0, half)))
    second_pair = projected_blocks([me ^ 1, me], later_queries)
    partner_own = lax.ppermute(second_pair[0].astype(jnp.bfloat16), "tp", xor_pairs(size, 1))
    projected = (
        second_pair[1]
        + partner_own.astype(jnp.float32)
        + from_across.astype(jnp.float32)
    )
    mixed = (residual_in.astype(jnp.float32) + projected).astype(jnp.bfloat16)
    normed = rms_norm(mixed, norm_gain)

    capacity = min(group_tokens * expert_ids.shape[1] * 5 // (EXPERTS * 4), group_tokens)
    window = gate_up.shape[0]
    slots = jnp.arange(window, dtype=jnp.int32)
    hits = expert_ids[:, :, None] == slots[None, None, :]
    route_all = jnp.sum(jnp.where(hits, gate_weights[:, :, None], 0.0), axis=1)
    chosen = jnp.any(hits, axis=1)
    rank = jnp.cumsum(chosen.astype(jnp.int32), axis=0) - 1
    kk = jnp.arange(-(-capacity // 8) * 8, dtype=jnp.int32)
    select_all = (rank.T[:, None, :] == kk[None, :, None]) & chosen.T[:, None, :]
    route_sel = jnp.sum(jnp.where(select_all, route_all.T[:, None, :], 0.0), axis=-1)
    select_loc = lax.dynamic_slice_in_dim(select_all, me * tok_rows, tok_rows, axis=2)

    picked = jnp.einsum(
        "ekt,td->ekd", select_loc.astype(jnp.bfloat16), normed,
        preferred_element_type=jnp.float32,
    ).astype(jnp.bfloat16)
    on_core = me % 2
    picked = picked + lax.ppermute(picked, "tp", xor_pairs(size, 1))
    mine = picked[on_core]
    mine = mine + lax.ppermute(mine, "tp", xor_pairs(size, 2))
    other = lax.ppermute(mine, "tp", xor_pairs(size, 1))
    picked = jnp.where(on_core == 0, jnp.stack([mine, other]), jnp.stack([other, mine]))
    gate = jnp.einsum("ekd,edf->ekf", picked, gate_up[:, 0], preferred_element_type=jnp.float32)
    upward = jnp.einsum("ekd,edf->ekf", picked, gate_up[:, 1], preferred_element_type=jnp.float32)
    active = (jax.nn.silu(gate) * upward).astype(jnp.bfloat16)
    outputs = jnp.einsum("ekf,efd->ekd", active, down_weight, preferred_element_type=jnp.float32)
    scaled = route_sel[:, :, None] * outputs
    scaled = scaled + lax.ppermute(scaled, "tp", xor_pairs(size, 1))
    mine = scaled[on_core]
    mine = mine + lax.ppermute(
        mine.astype(jnp.bfloat16), "tp", xor_pairs(size, 2)
    ).astype(jnp.float32)
    other = lax.ppermute(mine, "tp", xor_pairs(size, 1))
    scaled = jnp.where(on_core == 0, jnp.stack([mine, other]), jnp.stack([other, mine]))
    experts = jnp.einsum(
        "ekt,ekd->td", select_loc.astype(jnp.float32), scaled,
        precision=lax.Precision.HIGHEST, preferred_element_type=jnp.float32,
    )
    return (mixed.astype(jnp.float32) + experts).astype(jnp.bfloat16)


def solution(mesh):
    placed = (
        P("req", "tp"),
        P("req", "tp"),
        P("req", "tp"),
        P(("req", "tp"), None),
        P("tp", None),
        P(),
        P(None, None, None, "tp"),
        P(None, "tp", None),
        P("req"),
        P("req", None),
        P("req", None),
    )
    return jax.shard_map(
        local, mesh=mesh, in_specs=placed, out_specs=P(("req", "tp"), None), check_vma=False
    )
```

```python
import math

import jax
import jax.numpy as jnp
from jax import lax
from jax.sharding import PartitionSpec as P

QUERY_HEADS = 32
KEY_VALUE_HEADS = 4
HEAD_WIDTH = 128
EXPERTS = 128


def positions_of(segment_ids):
    earlier = (segment_ids[None, :] < segment_ids[:, None]).astype(jnp.int32)
    return jnp.arange(segment_ids.shape[0], dtype=jnp.int32) - jnp.sum(earlier, axis=1)


def rotary_tables(vectors, token_positions):
    half_dim = vectors.shape[-1] // 2
    frequency = 1000000.0 ** (-jnp.arange(half_dim, dtype=jnp.float32) / half_dim)
    angles = token_positions.astype(jnp.float32)[:, None] * frequency[None, :]
    cosine = jnp.cos(angles)[:, None, :]
    sine = jnp.sin(angles)[:, None, :]
    first = vectors[..., :half_dim]
    second = vectors[..., half_dim:]
    return jnp.concatenate(
        [first * cosine - second * sine, second * cosine + first * sine], axis=-1
    )


def rms_norm(hidden, gain):
    widened = hidden.astype(jnp.float32)
    factor = lax.rsqrt(jnp.mean(widened * widened, axis=-1, keepdims=True) + 1e-06)
    return (widened * factor * gain).astype(jnp.bfloat16)


SEG_MOST = 480


def xor_pairs(size, mask):
    return [(index, index ^ mask) for index in range(size)]


def attend_blocks(query_heads, firsts, rows, keys_after_rotary, values, segment_ids, token_positions):
    item_count = segment_ids.shape[0]
    span = min(item_count, rows + SEG_MOST)
    head_count = query_heads.shape[1] // HEAD_WIDTH
    starts = [jnp.clip(first + rows - span, 0, item_count - span) for first in firsts]
    row_index = jnp.stack([first + jnp.arange(rows, dtype=jnp.int32) for first in firsts])
    key_index = jnp.stack([start + jnp.arange(span, dtype=jnp.int32) for start in starts])
    row_segment = jnp.stack([lax.dynamic_slice_in_dim(segment_ids, f, rows) for f in firsts])
    key_segment = jnp.stack([lax.dynamic_slice_in_dim(segment_ids, s, span) for s in starts])
    key_one = jnp.stack([lax.dynamic_slice_in_dim(keys_after_rotary, s, span) for s in starts])
    value_one = jnp.stack([lax.dynamic_slice_in_dim(values, s, span) for s in starts])
    query_rows = jnp.concatenate([lax.dynamic_slice_in_dim(query_heads, f, rows) for f in firsts])
    row_positions = jnp.concatenate(
        [lax.dynamic_slice_in_dim(token_positions, f, rows) for f in firsts]
    )
    queries = rotary_tables(
        query_rows.reshape(len(firsts) * rows, head_count, HEAD_WIDTH).astype(jnp.float32),
        row_positions,
    ).astype(jnp.bfloat16)
    factor = 1.0 / math.sqrt(HEAD_WIDTH)
    stacked = queries.reshape(len(firsts), rows * head_count, HEAD_WIDTH)
    scores = jnp.einsum(
        "nqd,nkd->nqk", stacked, key_one, preferred_element_type=jnp.float32
    ) * factor
    stacked_segment = jnp.repeat(row_segment, head_count, axis=1)
    stacked_index = jnp.repeat(row_index, head_count, axis=1)
    allowed = (stacked_segment[:, :, None] == key_segment[:, None, :]) & (
        key_index[:, None, :] <= stacked_index[:, :, None]
    )
    scores = jnp.where(allowed, scores, -1e30)
    peak = jnp.max(scores, axis=2, keepdims=True)
    weights = jnp.exp(scores - peak)
    weights = (weights / jnp.sum(weights, axis=2, keepdims=True)).astype(jnp.bfloat16)
    attended = jnp.einsum(
        "nqk,nkd->nqd",
        weights,
        value_one,
        preferred_element_type=jnp.float32,
    ).astype(jnp.bfloat16)
    return attended.reshape(len(firsts), rows, head_count, HEAD_WIDTH)


def local(
    query_heads,
    normed_key_heads,
    value_rows_per_head,
    residual_in,
    out_weight,
    norm_gain,
    gate_up,
    down_weight,
    segment_ids,
    expert_ids,
    gate_weights,
):
    tok_rows = residual_in.shape[0]
    group_tokens = expert_ids.shape[0]
    size = lax.axis_size("tp")
    me = lax.axis_index("tp")
    token_positions = positions_of(segment_ids)
    keys_after_rotary = rotary_tables(
        normed_key_heads.reshape(group_tokens, 1, HEAD_WIDTH).astype(jnp.float32), token_positions
    ).astype(jnp.bfloat16)[:, 0]
    values = value_rows_per_head

    def projected_blocks(blocks, queries):
        attended = attend_blocks(
            queries, [block * tok_rows for block in blocks], tok_rows,
            keys_after_rotary, values, segment_ids, token_positions,
        )
        return jnp.einsum(
            "nrhc,hcd->nrd", attended, out_weight.reshape(attended.shape[2], HEAD_WIDTH, -1),
            preferred_element_type=jnp.float32,
        )

    first_pair = projected_blocks([me ^ 3, me ^ 2], query_heads)
    partner_cross = lax.ppermute(first_pair[0].astype(jnp.bfloat16), "tp", xor_pairs(size, 1))
    across = first_pair[1] + partner_cross.astype(jnp.float32)
    high = across.astype(jnp.bfloat16)
    half = across.shape[1] // 2
    low = (across[:, :half] - high[:, :half].astype(jnp.float32)).astype(jnp.bfloat16)
    message, later_queries = lax.optimization_barrier(
        (jnp.concatenate([high, low], axis=1), query_heads)
    )
    message = lax.ppermute(message, "tp", xor_pairs(size, 2)).astype(jnp.float32)
    from_across = message[:, : 2 * half] + jnp.pad(message[:, 2 * half :], ((0, 0), (0, half)))
    second_pair = projected_blocks([me ^ 1, me], later_queries)
    partner_own = lax.ppermute(second_pair[0].astype(jnp.bfloat16), "tp", xor_pairs(size, 1))
    projected = (
        second_pair[1]
        + partner_own.astype(jnp.float32)
        + from_across.astype(jnp.float32)
    )
    mixed = (residual_in.astype(jnp.float32) + projected).astype(jnp.bfloat16)
    normed = rms_norm(mixed, norm_gain)

    capacity = min(group_tokens * expert_ids.shape[1] * 5 // (EXPERTS * 4), group_tokens)
    window = gate_up.shape[0]
    slots = jnp.arange(window, dtype=jnp.int32)
    hits = expert_ids[:, :, None] == slots[None, None, :]
    route_all = jnp.sum(jnp.where(hits, gate_weights[:, :, None], 0.0), axis=1)
    chosen = jnp.any(hits, axis=1)
    rank = jnp.cumsum(chosen.astype(jnp.int32), axis=0) - 1
    kk = jnp.arange(-(-capacity // 8) * 8, dtype=jnp.int32)
    select_all = (rank.T[:, None, :] == kk[None, :, None]) & chosen.T[:, None, :]
    route_sel = jnp.sum(jnp.where(select_all, route_all.T[:, None, :], 0.0), axis=-1)
    select_loc = lax.dynamic_slice_in_dim(select_all, me * tok_rows, tok_rows, axis=2)

    picked = jnp.einsum(
        "ekt,td->ekd", select_loc.astype(jnp.bfloat16), normed,
        preferred_element_type=jnp.float32,
    ).astype(jnp.bfloat16)
    on_core = me % 2
    mine = picked[on_core] + lax.ppermute(picked[1 - on_core], "tp", xor_pairs(size, 1))
    mine = mine + lax.ppermute(mine, "tp", xor_pairs(size, 2))
    other = lax.ppermute(mine, "tp", xor_pairs(size, 1))
    picked = jnp.where(on_core == 0, jnp.stack([mine, other]), jnp.stack([other, mine]))
    gate = jnp.einsum("ekd,edf->ekf", picked, gate_up[:, 0], preferred_element_type=jnp.float32)
    upward = jnp.einsum("ekd,edf->ekf", picked, gate_up[:, 1], preferred_element_type=jnp.float32)
    active = (jax.nn.silu(gate) * upward).astype(jnp.bfloat16)
    outputs = jnp.einsum("ekf,efd->ekd", active, down_weight, preferred_element_type=jnp.float32)
    scaled = route_sel[:, :, None] * outputs
    mine = scaled[on_core] + lax.ppermute(scaled[1 - on_core], "tp", xor_pairs(size, 1))
    mine = mine + lax.ppermute(
        mine.astype(jnp.bfloat16), "tp", xor_pairs(size, 2)
    ).astype(jnp.float32)
    other = lax.ppermute(mine, "tp", xor_pairs(size, 1))
    scaled = jnp.where(on_core == 0, jnp.stack([mine, other]), jnp.stack([other, mine]))
    experts = jnp.einsum(
        "ekt,ekd->td", select_loc.astype(jnp.float32), scaled,
        precision=lax.Precision.HIGHEST, preferred_element_type=jnp.float32,
    )
    return (mixed.astype(jnp.float32) + experts).astype(jnp.bfloat16)


def solution(mesh):
    placed = (
        P("req", "tp"),
        P("req", "tp"),
        P("req", "tp"),
        P(("req", "tp"), None),
        P("tp", None),
        P(),
        P(None, None, None, "tp"),
        P(None, "tp", None),
        P("req"),
        P("req", None),
        P("req", None),
    )
    return jax.shard_map(
        local, mesh=mesh, in_specs=placed, out_specs=P(("req", "tp"), None), check_vma=False
    )
```
